32 devices in a mesh: scan: 16 (over z, y, core), row: 2 (over x).
Axes of the slice: x: 2, y: 2, z: 4, core: 2. Of those that a mesh axis runs over, the one named last changes fastest.
Arguments:
- estimate: float32 [128, 64, 512], P('scan', 'row'), may hold values from -6 to 6
- raw: float32 [128, 64, 512], P('scan', 'row'), may hold values from -6 to 6
- offsets: int32 [128], replicated, may hold values from 0 to 16, as said below
- depth_psf: float32 [64], replicated, may hold values from 0.03 to 0.2
- lateral_psf: float32 [17], replicated, may hold values from 0.05 to 0.4
- step_size: float32 [1], replicated, may hold values from 0.3 to 0.8
- threshold: float32 [1], replicated, may hold values from 0.3 to 1.5
Outputs:
- new_estimate: float32 [128, 64, 512], P('scan', 'row')
- misfit: float32 [128, 64, 512], P('scan', 'row')
The draws below stay inside these ranges and needn't reach their ends.
Inputs may be any that keep to these rules, and one draw needn't show every extreme that they name: offsets[p] is how many planes beyond p the sheet of scan plane p begins; both 0 and 16 occur.
All inputs are finite; a program needn't handle non-finite values.
Results may differ from the reference program's by a relative error of at most 0.0003.
Values sent between devices are 32-bit elements; how exact they have to be, the bound alone decides.
No kernel may reach another device: no remote copies, remote signals or barrier semaphores. Data moves between devices by JAX's collectives and lax.ppermute only.
A program may use at most 64 MiB of HBM per device.

```python
import math
import jax
import jax.numpy as jnp
from jax import lax

C = 512
K = 64
SHEAR = 16
PLANES = 128
ROWS = 64
TAPS = 17


def draw_offsets(key, part):
    first_key, second_key, third_key = jax.random.split(key, 3)
    sheet_shift = jax.random.randint(first_key, (PLANES,), 0, SHEAR + 1, dtype=jnp.int32)
    high_spot = jax.random.randint(second_key, (), 0, PLANES, dtype=jnp.int32)
    low_gap = jax.random.randint(third_key, (), 1, PLANES, dtype=jnp.int32)
    low_spot = (high_spot + low_gap) % PLANES
    sheet_shift = sheet_shift.at[high_spot].set(SHEAR)
    sheet_shift = sheet_shift.at[low_spot].set(0)
    return sheet_shift


def shard_levels(rng, extent, shards, low, largest):
    loudness = 1.0
    for position, shards_of in shards:
        heights = jax.random.uniform(jax.random.fold_in(jax.random.fold_in(rng, 6), position), (shards_of,), jnp.float32, low / len(shards), largest / len(shards))
        loudness = loudness * jnp.repeat(jnp.exp(heights), extent[position] // shards_of).reshape((-1,) + (1,) * (len(extent) - 1 - position))
    return loudness


def centred(key, extent, spread, most, pieces=(), kind=jnp.bfloat16):
    level = shard_levels(key, extent, pieces, -0.22, 0.18) if pieces else 1.0
    entries = jax.random.normal(key, extent, jnp.float32) * spread * level
    return jnp.minimum(jnp.maximum(entries, -most), most).astype(kind)


def setup_inputs(seed: int = 0) -> dict:
    splits = jax.random.split(jax.random.key(seed), 8)
    return {
        "estimate": centred(splits[0], (PLANES, ROWS, C), 1.0, 6.0, ((0, 16), (1, 2)), jnp.float32),
        "raw": centred(splits[1], (PLANES, ROWS, C), 1.0, 6.0, ((0, 16), (1, 2)), jnp.float32),
        "offsets": draw_offsets(jax.random.fold_in(splits[7], 71), 0),
        "depth_psf": jnp.clip(jnp.exp(jax.random.uniform(splits[3], (K,), jnp.float32, math.log(0.03), math.log(0.2))), 0.03, 0.2),
        "lateral_psf": jnp.clip(jnp.exp(jax.random.uniform(splits[4], (TAPS,), jnp.float32, math.log(0.05), math.log(0.4))), 0.05, 0.4),
        "step_size": jnp.clip(jnp.exp(jax.random.uniform(splits[5], (1,), jnp.float32, math.log(0.3), math.log(0.8))), 0.3, 0.8),
        "threshold": jnp.clip(jnp.exp(jax.random.uniform(splits[6], (1,), jnp.float32, math.log(0.3), math.log(1.5))), 0.3, 1.5),
    }


def lateral(volume, kernel_taps):
    halo_rows = kernel_taps.shape[0] // 2
    row_count = volume.shape[1]
    padded = jnp.pad(volume, ((0, 0), (halo_rows, halo_rows), (0, 0)))
    summed = jnp.zeros_like(volume)
    for tap_index in range(kernel_taps.shape[0]):
        summed = summed + kernel_taps[tap_index] * padded[:, tap_index:tap_index + row_count, :]
    return summed


def shear_matrix(offsets, depth_psf, plane_total):
    plane_ids = jnp.arange(plane_total, dtype=jnp.int32)
    lag_planes = plane_ids[None, :] - plane_ids[:, None] - offsets[:, None]
    depth_count = depth_psf.shape[0]
    inside = (lag_planes >= 0) & (lag_planes < depth_count)
    looked = jnp.take(depth_psf, jnp.clip(lag_planes, 0, depth_count - 1))
    return jnp.where(inside, looked, 0.0)


def reference(estimate, raw, offsets, depth_psf, lateral_psf, step_size, threshold):
    plane_total = estimate.shape[0]
    flat_count = estimate.shape[1] * estimate.shape[2]
    matrix = shear_matrix(offsets, depth_psf, plane_total)
    blurred = lateral(estimate, lateral_psf).reshape(plane_total, flat_count)
    predicted = jnp.dot(matrix, blurred, precision=lax.Precision.HIGHEST)
    misfit = predicted - raw.reshape(plane_total, flat_count)
    back_flat = lax.dot_general(matrix, misfit, (((0,), (0,)), ((), ())), precision=lax.Precision.HIGHEST)
    gradient = lateral(back_flat.reshape(estimate.shape), lateral_psf[::-1])
    stepped = estimate - step_size[0] * gradient
    shrink_level = step_size[0] * threshold[0]
    new_estimate = jnp.sign(stepped) * jnp.maximum(jnp.abs(stepped) - shrink_level, 0.0)
    return new_estimate, misfit.reshape(estimate.shape)
```

```python
import jax
import jax.numpy as jnp
from jax import lax
from jax.sharding import PartitionSpec as P

highest_mode = lax.Precision.HIGHEST


def with_halo(cells, sides, width):
    for axis, dim in sides:
        count = lax.axis_size(axis)
        ends = count - 1
        head = lax.slice_in_dim(cells, 0, width, axis=dim)
        tail = lax.slice_in_dim(cells, cells.shape[dim] - width, cells.shape[dim], axis=dim)
        cells = jnp.concatenate(
            [
                lax.ppermute(tail, axis, [(i, (i + 1) % count) for i in range(ends)]),
                cells,
                lax.ppermute(head, axis, [((i + 1) % count, i) for i in range(ends)]),
            ],
            axis=dim,
        )
    return cells


def lateral_blur(padded, kernel_taps, row_count):
    summed = jnp.zeros((padded.shape[0], row_count, padded.shape[2]), jnp.float32)
    for tap_index in range(kernel_taps.shape[0]):
        summed = summed + kernel_taps[tap_index] * padded[:, tap_index : tap_index + row_count, :]
    return summed


def sheet_matrix(own_offsets, depth_psf, column_count):
    plane_rows = jnp.arange(own_offsets.shape[0], dtype=jnp.int32)[:, None]
    plane_columns = jnp.arange(column_count, dtype=jnp.int32)[None, :]
    lag_planes = plane_columns - plane_rows - own_offsets[:, None]
    depth_count = depth_psf.shape[0]
    inside = (lag_planes >= 0) & (lag_planes < depth_count)
    taps = jnp.arange(depth_count, dtype=jnp.int32)
    picked = jnp.where(lag_planes[:, :, None] == taps, depth_psf, 0.0)
    return jnp.where(inside, jnp.sum(picked, axis=-1), 0.0)


def transpose_apply(sheet_psf, values):
    return lax.dot_general(sheet_psf, values, (((0,), (0,)), ((), ())), precision=highest_mode)


def body(estimate, raw, offsets, depth_psf, lateral_psf, step_size, threshold):
    plane_count, row_count, width_count = estimate.shape
    flat_count = row_count * width_count
    halo_rows = lateral_psf.shape[0] // 2
    padded = with_halo(estimate, (("row", 1),), halo_rows)
    blurred = lateral_blur(padded, lateral_psf, row_count).reshape(plane_count, flat_count)
    raw_flat = raw.reshape(plane_count, flat_count)
    sheet_psf = sheet_matrix(offsets, depth_psf, offsets.shape[0])
    pencil = lax.all_to_all(blurred, "scan", split_axis=1, concat_axis=0, tiled=True)
    predicted_pencil = jnp.dot(sheet_psf, pencil, precision=highest_mode)
    predicted = lax.all_to_all(predicted_pencil, "scan", split_axis=0, concat_axis=1, tiled=True)
    misfit = predicted - raw_flat
    misfit_pencil = lax.all_to_all(misfit, "scan", split_axis=1, concat_axis=0, tiled=True)
    back_pencil = transpose_apply(sheet_psf, misfit_pencil)
    back_flat = lax.all_to_all(back_pencil, "scan", split_axis=0, concat_axis=1, tiled=True)
    back_volume = back_flat.reshape(plane_count, row_count, width_count)
    padded_back = with_halo(back_volume, (("row", 1),), halo_rows)
    gradient = lateral_blur(padded_back, lateral_psf[::-1], row_count)
    stepped = estimate - step_size[0] * gradient
    shrink_level = step_size[0] * threshold[0]
    new_estimate = jnp.sign(stepped) * jnp.maximum(jnp.abs(stepped) - shrink_level, 0.0)
    return (new_estimate, misfit.reshape(plane_count, row_count, width_count))


def solution(mesh):
    placed = (P("scan", "row", None), P("scan", "row", None), P(), P(), P(), P(), P())
    return jax.shard_map(
        body,
        mesh=mesh,
        in_specs=placed,
        out_specs=(P("scan", "row", None), P("scan", "row", None)),
        check_vma=False,
    )
```

```python
import jax
import jax.numpy as jnp
from jax import lax
from jax.sharding import PartitionSpec as P

highest_mode = lax.Precision.HIGHEST


def with_halo(cells, sides, width):
    for axis, dim in sides:
        count = lax.axis_size(axis)
        ends = count - 1
        head = lax.slice_in_dim(cells, 0, width, axis=dim)
        tail = lax.slice_in_dim(cells, cells.shape[dim] - width, cells.shape[dim], axis=dim)
        cells = jnp.concatenate(
            [
                lax.ppermute(tail, axis, [(i, (i + 1) % count) for i in range(ends)]),
                cells,
                lax.ppermute(head, axis, [((i + 1) % count, i) for i in range(ends)]),
            ],
            axis=dim,
        )
    return cells


def band_matrix(kernel_taps, row_count, shift):
    tap_count = kernel_taps.shape[0]
    out_rows = jnp.arange(row_count, dtype=jnp.int32)[:, None]
    in_rows = jnp.arange(row_count + tap_count - 1, dtype=jnp.int32)[None, :]
    lag = shift + in_rows - out_rows
    taps = jnp.arange(tap_count, dtype=jnp.int32)
    return jnp.sum(jnp.where(lag[:, :, None] == taps, kernel_taps, 0.0), axis=-1)


def lateral_apply(band, padded):
    return jnp.einsum("rk,pkc->prc", band, padded, precision=highest_mode)


def sheet_matrix(own_offsets, depth_psf, column_count):
    plane_rows = jnp.arange(own_offsets.shape[0], dtype=jnp.int32)[:, None]
    plane_columns = jnp.arange(column_count, dtype=jnp.int32)[None, :]
    lag_planes = plane_columns - plane_rows - own_offsets[:, None]
    depth_count = depth_psf.shape[0]
    inside = (lag_planes >= 0) & (lag_planes < depth_count)
    taps = jnp.arange(depth_count, dtype=jnp.int32)
    picked = jnp.where(lag_planes[:, :, None] == taps, depth_psf, 0.0)
    return jnp.where(inside, jnp.sum(picked, axis=-1), 0.0)


def transpose_apply(sheet_psf, values):
    return lax.dot_general(sheet_psf, values, (((0,), (0,)), ((), ())), precision=highest_mode)


def body(estimate, raw, offsets, depth_psf, lateral_psf, step_size, threshold):
    plane_count, row_count, width_count = estimate.shape
    flat_count = row_count * width_count
    halo_rows = lateral_psf.shape[0] // 2
    raw_pencil = lax.all_to_all(raw.reshape(plane_count, flat_count), "scan", split_axis=1, concat_axis=0, tiled=True)
    sheet_psf = sheet_matrix(offsets, depth_psf, offsets.shape[0])
    blur_band = band_matrix(lateral_psf, row_count, 0)
    back_band = band_matrix(lateral_psf[::-1], row_count, 0)
    padded = with_halo(estimate, (("row", 1),), halo_rows)
    blurred = lateral_apply(blur_band, padded).reshape(plane_count, flat_count)
    pencil = lax.all_to_all(blurred, "scan", split_axis=1, concat_axis=0, tiled=True)
    predicted_pencil = jnp.dot(sheet_psf, pencil, precision=highest_mode)
    misfit_pencil = predicted_pencil - raw_pencil
    back_pencil = transpose_apply(sheet_psf, misfit_pencil)
    both_pencil = jnp.stack([misfit_pencil, back_pencil])
    both = lax.all_to_all(both_pencil, "scan", split_axis=1, concat_axis=2, tiled=True)
    misfit = both[0]
    back_volume = both[1].reshape(plane_count, row_count, width_count)
    padded_back = with_halo(back_volume, (("row", 1),), halo_rows)
    gradient = lateral_apply(back_band, padded_back)
    stepped = estimate - step_size[0] * gradient
    shrink_level = step_size[0] * threshold[0]
    new_estimate = jnp.sign(stepped) * jnp.maximum(jnp.abs(stepped) - shrink_level, 0.0)
    return (new_estimate, misfit.reshape(plane_count, row_count, width_count))


def solution(mesh):
    placed = (P("scan", "row", None), P("scan", "row", None), P(), P(), P(), P(), P())
    return jax.shard_map(
        body,
        mesh=mesh,
        in_specs=placed,
        out_specs=(P("scan", "row", None), P("scan", "row", None)),
        check_vma=False,
    )
```

```python
import jax
import jax.numpy as jnp
from jax import lax
from jax.sharding import PartitionSpec as P

highest_mode = lax.Precision.HIGHEST
both_axes = ("scan", "row")


def band_matrix(kernel_taps, row_count):
    tap_count = kernel_taps.shape[0]
    half = tap_count // 2
    out_rows = jnp.arange(row_count, dtype=jnp.int32)[:, None]
    in_rows = jnp.arange(row_count, dtype=jnp.int32)[None, :]
    lag = in_rows - out_rows + half
    taps = jnp.arange(tap_count, dtype=jnp.int32)
    return jnp.sum(jnp.where(lag[:, :, None] == taps, kernel_taps, 0.0), axis=-1)


def sheet_matrix(own_offsets, depth_psf, column_count):
    plane_rows = jnp.arange(own_offsets.shape[0], dtype=jnp.int32)[:, None]
    plane_columns = jnp.arange(column_count, dtype=jnp.int32)[None, :]
    lag_planes = plane_columns - plane_rows - own_offsets[:, None]
    depth_count = depth_psf.shape[0]
    inside = (lag_planes >= 0) & (lag_planes < depth_count)
    taps = jnp.arange(depth_count, dtype=jnp.int32)
    picked = jnp.where(lag_planes[:, :, None] == taps, depth_psf, 0.0)
    return jnp.where(inside, jnp.sum(picked, axis=-1), 0.0)


def body(estimate, raw, offsets, depth_psf, lateral_psf, step_size, threshold):
    plane_count, row_count, width_count = estimate.shape
    scan_count = lax.axis_size("scan")
    row_split = lax.axis_size("row")
    pencil_count = scan_count * row_split
    strip = width_count // pencil_count
    all_planes = scan_count * plane_count
    all_rows = row_split * row_count

    def chunked(volume):
        parts = volume.reshape(plane_count, row_count, pencil_count, strip)
        return parts.transpose(2, 0, 1, 3).reshape(pencil_count, plane_count, row_count * strip)

    outgoing = jnp.stack([chunked(estimate), chunked(raw)], axis=1)
    incoming = lax.all_to_all(outgoing, both_axes, split_axis=0, concat_axis=0, tiled=True)
    incoming = incoming.reshape(scan_count, row_split, 2, plane_count, row_count, strip)
    pencils = incoming.transpose(2, 1, 4, 5, 0, 3).reshape(2, all_rows, strip * all_planes)
    est_pencil = pencils[0]
    raw_pencil = pencils[1].reshape(all_rows * strip, all_planes)

    band = band_matrix(lateral_psf, all_rows)
    sheet_psf = sheet_matrix(offsets, depth_psf, offsets.shape[0])
    blurred = jnp.dot(band, est_pencil, precision=highest_mode).reshape(all_rows * strip, all_planes)
    predicted = lax.dot_general(blurred, sheet_psf, (((1,), (1,)), ((), ())), precision=highest_mode)
    misfit_pencil = predicted - raw_pencil
    back = jnp.dot(misfit_pencil, sheet_psf, precision=highest_mode).reshape(all_rows, strip * all_planes)
    gradient = lax.dot_general(band, back, (((0,), (0,)), ((), ())), precision=highest_mode)
    stepped = est_pencil - step_size[0] * gradient
    shrink_level = step_size[0] * threshold[0]
    new_pencil = jnp.sign(stepped) * jnp.maximum(jnp.abs(stepped) - shrink_level, 0.0)

    results = jnp.stack([new_pencil.reshape(all_rows * strip, all_planes), misfit_pencil])
    results = results.reshape(2, row_split, row_count, strip, scan_count, plane_count)
    results = results.transpose(4, 1, 0, 5, 2, 3).reshape(pencil_count, 2, plane_count, row_count * strip)
    homes = lax.all_to_all(results, both_axes, split_axis=0, concat_axis=0, tiled=True)
    homes = homes.reshape(pencil_count, 2, plane_count, row_count, strip)
    homes = homes.transpose(1, 2, 3, 0, 4).reshape(2, plane_count, row_count, width_count)
    return (homes[0], homes[1])


def solution(mesh):
    placed = (P("scan", "row", None), P("scan", "row", None), P(), P(), P(), P(), P())
    return jax.shard_map(
        body,
        mesh=mesh,
        in_specs=placed,
        out_specs=(P("scan", "row", None), P("scan", "row", None)),
        check_vma=False,
    )
```

```python
import jax
import jax.numpy as jnp
from jax import lax
from jax.sharding import PartitionSpec as P

highest_mode = lax.Precision.HIGHEST


def with_halo(cells, axis, width):
    count = lax.axis_size(axis)
    head = lax.slice_in_dim(cells, 0, width, axis=1)
    tail = lax.slice_in_dim(cells, cells.shape[1] - width, cells.shape[1], axis=1)
    zeros = jnp.zeros_like(head)
    if count == 2:
        first = lax.axis_index(axis) == 0
        arrived = lax.ppermute(jnp.where(first, tail, head), axis, [(0, 1), (1, 0)])
        above = jnp.where(first, zeros, arrived)
        below = jnp.where(first, arrived, zeros)
    else:
        ends = count - 1
        above = lax.ppermute(tail, axis, [(i, (i + 1) % count) for i in range(ends)])
        below = lax.ppermute(head, axis, [((i + 1) % count, i) for i in range(ends)])
    return jnp.concatenate([above, cells, below], axis=1)


def band_matrix(kernel_taps, row_count, shift):
    tap_count = kernel_taps.shape[0]
    out_rows = jnp.arange(row_count, dtype=jnp.int32)[:, None]
    in_rows = jnp.arange(row_count + tap_count - 1, dtype=jnp.int32)[None, :]
    lag = shift + in_rows - out_rows
    taps = jnp.arange(tap_count, dtype=jnp.int32)
    return jnp.sum(jnp.where(lag[:, :, None] == taps, kernel_taps, 0.0), axis=-1)


def lateral_apply(band, padded):
    return jnp.einsum("rk,pkc->prc", band, padded, precision=highest_mode)


def sheet_matrix(own_offsets, depth_psf, column_count):
    plane_rows = jnp.arange(own_offsets.shape[0], dtype=jnp.int32)[:, None]
    plane_columns = jnp.arange(column_count, dtype=jnp.int32)[None, :]
    lag_planes = plane_columns - plane_rows - own_offsets[:, None]
    depth_count = depth_psf.shape[0]
    inside = (lag_planes >= 0) & (lag_planes < depth_count)
    taps = jnp.arange(depth_count, dtype=jnp.int32)
    picked = jnp.where(lag_planes[:, :, None] == taps, depth_psf, 0.0)
    return jnp.where(inside, jnp.sum(picked, axis=-1), 0.0)


def transpose_apply(sheet_psf, values):
    return lax.dot_general(sheet_psf, values, (((0,), (0,)), ((), ())), precision=highest_mode)


def body(estimate, raw, offsets, depth_psf, lateral_psf, step_size, threshold):
    plane_count, row_count, width_count = estimate.shape
    flat_count = row_count * width_count
    halo_rows = lateral_psf.shape[0] // 2
    raw_pencil = lax.all_to_all(raw.reshape(plane_count, flat_count), "scan", split_axis=1, concat_axis=0, tiled=True)
    sheet_psf = sheet_matrix(offsets, depth_psf, offsets.shape[0])
    blur_band = band_matrix(lateral_psf, row_count, 0)
    back_band = band_matrix(lateral_psf[::-1], row_count, 0)
    padded = with_halo(estimate, "row", halo_rows)
    blurred = lateral_apply(blur_band, padded).reshape(plane_count, flat_count)
    pencil = lax.all_to_all(blurred, "scan", split_axis=1, concat_axis=0, tiled=True)
    predicted_pencil = jnp.dot(sheet_psf, pencil, precision=highest_mode)
    misfit_pencil = predicted_pencil - raw_pencil
    back_pencil = transpose_apply(sheet_psf, misfit_pencil)
    back_flat = lax.all_to_all(back_pencil, "scan", split_axis=0, concat_axis=1, tiled=True)
    misfit = lax.all_to_all(misfit_pencil, "scan", split_axis=0, concat_axis=1, tiled=True)
    back_volume = back_flat.reshape(plane_count, row_count, width_count)
    padded_back = with_halo(back_volume, "row", halo_rows)
    gradient = lateral_apply(back_band, padded_back)
    stepped = estimate - step_size[0] * gradient
    shrink_level = step_size[0] * threshold[0]
    new_estimate = jnp.sign(stepped) * jnp.maximum(jnp.abs(stepped) - shrink_level, 0.0)
    return (new_estimate, misfit.reshape(plane_count, row_count, width_count))


def solution(mesh):
    placed = (P("scan", "row", None), P("scan", "row", None), P(), P(), P(), P(), P())
    return jax.shard_map(
        body,
        mesh=mesh,
        in_specs=placed,
        out_specs=(P("scan", "row", None), P("scan", "row", None)),
        check_vma=False,
    )
```

```python
import jax
import jax.numpy as jnp
from jax import lax
from jax.sharding import PartitionSpec as P

highest_mode = lax.Precision.HIGHEST


def with_halo(cells, axis, width):
    count = lax.axis_size(axis)
    head = lax.slice_in_dim(cells, 0, width, axis=1)
    tail = lax.slice_in_dim(cells, cells.shape[1] - width, cells.shape[1], axis=1)
    zeros = jnp.zeros_like(head)
    if count == 2:
        first = lax.axis_index(axis) == 0
        arrived = lax.ppermute(jnp.where(first, tail, head), axis, [(0, 1), (1, 0)])
        above = jnp.where(first, zeros, arrived)
        below = jnp.where(first, arrived, zeros)
    else:
        ends = count - 1
        above = lax.ppermute(tail, axis, [(i, (i + 1) % count) for i in range(ends)])
        below = lax.ppermute(head, axis, [((i + 1) % count, i) for i in range(ends)])
    return jnp.concatenate([above, cells, below], axis=1)


def band_matrix(kernel_taps, row_count, shift):
    tap_count = kernel_taps.shape[0]
    out_rows = jnp.arange(row_count, dtype=jnp.int32)[:, None]
    in_rows = jnp.arange(row_count + tap_count - 1, dtype=jnp.int32)[None, :]
    lag = shift + in_rows - out_rows
    taps = jnp.arange(tap_count, dtype=jnp.int32)
    return jnp.sum(jnp.where(lag[:, :, None] == taps, kernel_taps, 0.0), axis=-1)


def lateral_apply(band, padded):
    return jnp.einsum("rk,pkc->prc", band, padded, precision=highest_mode)


def sheet_matrix(own_offsets, depth_psf, column_count):
    plane_rows = jnp.arange(own_offsets.shape[0], dtype=jnp.int32)[:, None]
    plane_columns = jnp.arange(column_count, dtype=jnp.int32)[None, :]
    lag_planes = plane_columns - plane_rows - own_offsets[:, None]
    depth_count = depth_psf.shape[0]
    inside = (lag_planes >= 0) & (lag_planes < depth_count)
    taps = jnp.arange(depth_count, dtype=jnp.int32)
    picked = jnp.where(lag_planes[:, :, None] == taps, depth_psf, 0.0)
    return jnp.where(inside, jnp.sum(picked, axis=-1), 0.0)


def transpose_apply(sheet_psf, values):
    return lax.dot_general(sheet_psf, values, (((0,), (0,)), ((), ())), precision=highest_mode)


def body(estimate, raw, offsets, depth_psf, lateral_psf, step_size, threshold):
    plane_count, row_count, width_count = estimate.shape
    flat_count = row_count * width_count
    halo_rows = lateral_psf.shape[0] // 2
    sheet_psf = sheet_matrix(offsets, depth_psf, offsets.shape[0])
    blur_band = band_matrix(lateral_psf, row_count, 0)
    back_band = band_matrix(lateral_psf[::-1], row_count, 0)
    padded = with_halo(estimate, "row", halo_rows)
    blurred = lateral_apply(blur_band, padded).reshape(plane_count, flat_count)
    both_flat = jnp.stack([blurred, raw.reshape(plane_count, flat_count)])
    both_in = lax.all_to_all(both_flat, "scan", split_axis=2, concat_axis=1, tiled=True)
    pencil = both_in[0]
    raw_pencil = both_in[1]
    predicted_pencil = jnp.dot(sheet_psf, pencil, precision=highest_mode)
    misfit_pencil = predicted_pencil - raw_pencil
    back_pencil = transpose_apply(sheet_psf, misfit_pencil)
    both_out = lax.all_to_all(jnp.stack([misfit_pencil, back_pencil]), "scan", split_axis=1, concat_axis=2, tiled=True)
    misfit = both_out[0]
    back_volume = both_out[1].reshape(plane_count, row_count, width_count)
    padded_back = with_halo(back_volume, "row", halo_rows)
    gradient = lateral_apply(back_band, padded_back)
    stepped = estimate - step_size[0] * gradient
    shrink_level = step_size[0] * threshold[0]
    new_estimate = jnp.sign(stepped) * jnp.maximum(jnp.abs(stepped) - shrink_level, 0.0)
    return (new_estimate, misfit.reshape(plane_count, row_count, width_count))


def solution(mesh):
    placed = (P("scan", "row", None), P("scan", "row", None), P(), P(), P(), P(), P())
    return jax.shard_map(
        body,
        mesh=mesh,
        in_specs=placed,
        out_specs=(P("scan", "row", None), P("scan", "row", None)),
        check_vma=False,
    )
```

```python
import jax
import jax.numpy as jnp
from jax import lax
from jax.sharding import PartitionSpec as P

highest_mode = lax.Precision.HIGHEST


def with_halo(cells, axis, width):
    count = lax.axis_size(axis)
    head = lax.slice_in_dim(cells, 0, width, axis=1)
    tail = lax.slice_in_dim(cells, cells.shape[1] - width, cells.shape[1], axis=1)
    zeros = jnp.zeros_like(head)
    if count == 2:
        first = lax.axis_index(axis) == 0
        arrived = lax.ppermute(jnp.where(first, tail, head), axis, [(0, 1), (1, 0)])
        above = jnp.where(first, zeros, arrived)
        below = jnp.where(first, arrived, zeros)
    else:
        ends = count - 1
        above = lax.ppermute(tail, axis, [(i, (i + 1) % count) for i in range(ends)])
        below = lax.ppermute(head, axis, [((i + 1) % count, i) for i in range(ends)])
    return jnp.concatenate([above, cells, below], axis=1)


def band_matrix(kernel_taps, row_count, shift):
    tap_count = kernel_taps.shape[0]
    out_rows = jnp.arange(row_count, dtype=jnp.int32)[:, None]
    in_rows = jnp.arange(row_count + tap_count - 1, dtype=jnp.int32)[None, :]
    lag = shift + in_rows - out_rows
    taps = jnp.arange(tap_count, dtype=jnp.int32)
    return jnp.sum(jnp.where(lag[:, :, None] == taps, kernel_taps, 0.0), axis=-1)


def lateral_apply(band, padded):
    return jnp.einsum("rk,pkc->prc", band, padded, precision=highest_mode)


def sheet_matrix(own_offsets, depth_psf, column_count):
    plane_rows = jnp.arange(own_offsets.shape[0], dtype=jnp.int32)[:, None]
    plane_columns = jnp.arange(column_count, dtype=jnp.int32)[None, :]
    lag_planes = plane_columns - plane_rows - own_offsets[:, None]
    depth_count = depth_psf.shape[0]
    inside = (lag_planes >= 0) & (lag_planes < depth_count)
    taps = jnp.arange(depth_count, dtype=jnp.int32)
    picked = jnp.where(lag_planes[:, :, None] == taps, depth_psf, 0.0)
    return jnp.where(inside, jnp.sum(picked, axis=-1), 0.0)


def transpose_apply(sheet_psf, values):
    return lax.dot_general(sheet_psf, values, (((0,), (0,)), ((), ())), precision=highest_mode)


def body(estimate, raw, offsets, depth_psf, lateral_psf, step_size, threshold):
    plane_count, row_count, width_count = estimate.shape
    flat_count = row_count * width_count
    halo_rows = lateral_psf.shape[0] // 2
    sheet_psf = sheet_matrix(offsets, depth_psf, offsets.shape[0])
    blur_band = band_matrix(lateral_psf, row_count, 0)
    back_band = band_matrix(lateral_psf[::-1], row_count, 0)
    padded = with_halo(estimate, "row", halo_rows)
    blurred = lateral_apply(blur_band, padded).reshape(plane_count, flat_count)
    both_flat = jnp.concatenate([blurred, raw.reshape(plane_count, flat_count)], axis=0)
    both_in = lax.all_to_all(both_flat, "scan", split_axis=1, concat_axis=0, tiled=True)
    both_in = both_in.reshape(lax.axis_size("scan"), 2, plane_count, -1)
    pencil = both_in[:, 0].reshape(offsets.shape[0], -1)
    raw_pencil = both_in[:, 1].reshape(offsets.shape[0], -1)
    predicted_pencil = jnp.dot(sheet_psf, pencil, precision=highest_mode)
    misfit_pencil = predicted_pencil - raw_pencil
    back_pencil = transpose_apply(sheet_psf, misfit_pencil)
    both_out = lax.all_to_all(jnp.stack([misfit_pencil, back_pencil]), "scan", split_axis=1, concat_axis=2, tiled=True)
    misfit = both_out[0]
    back_volume = both_out[1].reshape(plane_count, row_count, width_count)
    padded_back = with_halo(back_volume, "row", halo_rows)
    gradient = lateral_apply(back_band, padded_back)
    stepped = estimate - step_size[0] * gradient
    shrink_level = step_size[0] * threshold[0]
    new_estimate = jnp.sign(stepped) * jnp.maximum(jnp.abs(stepped) - shrink_level, 0.0)
    return (new_estimate, misfit.reshape(plane_count, row_count, width_count))


def solution(mesh):
    placed = (P("scan", "row", None), P("scan", "row", None), P(), P(), P(), P(), P())
    return jax.shard_map(
        body,
        mesh=mesh,
        in_specs=placed,
        out_specs=(P("scan", "row", None), P("scan", "row", None)),
        check_vma=False,
    )
```

```python
import jax
import jax.numpy as jnp
from jax import lax
from jax.sharding import PartitionSpec as P

highest_mode = lax.Precision.HIGHEST


def with_halo(cells, axis, width):
    count = lax.axis_size(axis)
    head = lax.slice_in_dim(cells, 0, width, axis=1)
    tail = lax.slice_in_dim(cells, cells.shape[1] - width, cells.shape[1], axis=1)
    zeros = jnp.zeros_like(head)
    if count == 2:
        first = lax.axis_index(axis) == 0
        arrived = lax.ppermute(jnp.where(first, tail, head), axis, [(0, 1), (1, 0)])
        above = jnp.where(first, zeros, arrived)
        below = jnp.where(first, arrived, zeros)
    else:
        ends = count - 1
        above = lax.ppermute(tail, axis, [(i, (i + 1) % count) for i in range(ends)])
        below = lax.ppermute(head, axis, [((i + 1) % count, i) for i in range(ends)])
    return jnp.concatenate([above, cells, below], axis=1)


def ring_exchange(chunks, axis):
    count = lax.axis_size(axis)
    me = lax.axis_index(axis)
    mine = lax.dynamic_index_in_dim(chunks, me, keepdims=False)
    result = lax.dynamic_update_index_in_dim(jnp.zeros_like(chunks), mine, me, axis=0)
    for shift in range(1, count):
        piece = lax.dynamic_index_in_dim(chunks, (me + shift) % count, keepdims=False)
        got = lax.ppermute(piece, axis, [(j, (j + shift) % count) for j in range(count)])
        result = lax.dynamic_update_index_in_dim(result, got, (me + count - shift) % count, axis=0)
    return result


def band_matrix(kernel_taps, row_count, shift):
    tap_count = kernel_taps.shape[0]
    out_rows = jnp.arange(row_count, dtype=jnp.int32)[:, None]
    in_rows = jnp.arange(row_count + tap_count - 1, dtype=jnp.int32)[None, :]
    lag = shift + in_rows - out_rows
    taps = jnp.arange(tap_count, dtype=jnp.int32)
    return jnp.sum(jnp.where(lag[:, :, None] == taps, kernel_taps, 0.0), axis=-1)


def lateral_apply(band, padded):
    return jnp.einsum("rk,pkc->prc", band, padded, precision=highest_mode)


def sheet_matrix(own_offsets, depth_psf, column_count):
    plane_rows = jnp.arange(own_offsets.shape[0], dtype=jnp.int32)[:, None]
    plane_columns = jnp.arange(column_count, dtype=jnp.int32)[None, :]
    lag_planes = plane_columns - plane_rows - own_offsets[:, None]
    depth_count = depth_psf.shape[0]
    inside = (lag_planes >= 0) & (lag_planes < depth_count)
    taps = jnp.arange(depth_count, dtype=jnp.int32)
    picked = jnp.where(lag_planes[:, :, None] == taps, depth_psf, 0.0)
    return jnp.where(inside, jnp.sum(picked, axis=-1), 0.0)


def transpose_apply(sheet_psf, values):
    return lax.dot_general(sheet_psf, values, (((0,), (0,)), ((), ())), precision=highest_mode)


def body(estimate, raw, offsets, depth_psf, lateral_psf, step_size, threshold):
    plane_count, row_count, width_count = estimate.shape
    flat_count = row_count * width_count
    halo_rows = lateral_psf.shape[0] // 2
    sheet_psf = sheet_matrix(offsets, depth_psf, offsets.shape[0])
    blur_band = band_matrix(lateral_psf, row_count, 0)
    back_band = band_matrix(lateral_psf[::-1], row_count, 0)
    padded = with_halo(estimate, "row", halo_rows)
    blurred = lateral_apply(blur_band, padded).reshape(plane_count, flat_count)
    scan_count = lax.axis_size("scan")
    both_flat = jnp.stack([blurred, raw.reshape(plane_count, flat_count)])
    outgoing = both_flat.reshape(2, plane_count, scan_count, flat_count // scan_count).transpose(2, 0, 1, 3)
    both_in = ring_exchange(outgoing, "scan")
    pencil = both_in[:, 0].reshape(offsets.shape[0], -1)
    raw_pencil = both_in[:, 1].reshape(offsets.shape[0], -1)
    predicted_pencil = jnp.dot(sheet_psf, pencil, precision=highest_mode)
    misfit_pencil = predicted_pencil - raw_pencil
    back_pencil = transpose_apply(sheet_psf, misfit_pencil)
    results = jnp.stack([misfit_pencil, back_pencil]).reshape(2, scan_count, plane_count, -1).transpose(1, 0, 2, 3)
    both_out = ring_exchange(results, "scan").transpose(1, 2, 0, 3).reshape(2, plane_count, flat_count)
    misfit = both_out[0]
    back_volume = both_out[1].reshape(plane_count, row_count, width_count)
    padded_back = with_halo(back_volume, "row", halo_rows)
    gradient = lateral_apply(back_band, padded_back)
    stepped = estimate - step_size[0] * gradient
    shrink_level = step_size[0] * threshold[0]
    new_estimate = jnp.sign(stepped) * jnp.maximum(jnp.abs(stepped) - shrink_level, 0.0)
    return (new_estimate, misfit.reshape(plane_count, row_count, width_count))


def solution(mesh):
    placed = (P("scan", "row", None), P("scan", "row", None), P(), P(), P(), P(), P())
    return jax.shard_map(
        body,
        mesh=mesh,
        in_specs=placed,
        out_specs=(P("scan", "row", None), P("scan", "row", None)),
        check_vma=False,
    )
```

```python
import jax
import jax.numpy as jnp
from jax import lax
from jax.sharding import PartitionSpec as P

highest_mode = lax.Precision.HIGHEST


def with_halo(cells, axis, width):
    count = lax.axis_size(axis)
    head = lax.slice_in_dim(cells, 0, width, axis=1)
    tail = lax.slice_in_dim(cells, cells.shape[1] - width, cells.shape[1], axis=1)
    zeros = jnp.zeros_like(head)
    if count == 2:
        first = lax.axis_index(axis) == 0
        arrived = lax.ppermute(jnp.where(first, tail, head), axis, [(0, 1), (1, 0)])
        above = jnp.where(first, zeros, arrived)
        below = jnp.where(first, arrived, zeros)
    else:
        ends = count - 1
        above = lax.ppermute(tail, axis, [(i, (i + 1) % count) for i in range(ends)])
        below = lax.ppermute(head, axis, [((i + 1) % count, i) for i in range(ends)])
    return jnp.concatenate([above, cells, below], axis=1)


def ring_exchange(chunks, axis):
    count = lax.axis_size(axis)
    me = lax.axis_index(axis)
    mine = lax.dynamic_index_in_dim(chunks, me, keepdims=False)
    result = lax.dynamic_update_index_in_dim(jnp.zeros_like(chunks), mine, me, axis=0)
    for shift in range(1, count):
        piece = lax.dynamic_index_in_dim(chunks, (me + shift) % count, keepdims=False)
        got = lax.ppermute(piece, axis, [(j, (j + shift) % count) for j in range(count)])
        result = lax.dynamic_update_index_in_dim(result, got, (me + count - shift) % count, axis=0)
    return result


def band_matrix(kernel_taps, row_count, shift):
    tap_count = kernel_taps.shape[0]
    out_rows = jnp.arange(row_count, dtype=jnp.int32)[:, None]
    in_rows = jnp.arange(row_count + tap_count - 1, dtype=jnp.int32)[None, :]
    lag = shift + in_rows - out_rows
    taps = jnp.arange(tap_count, dtype=jnp.int32)
    return jnp.sum(jnp.where(lag[:, :, None] == taps, kernel_taps, 0.0), axis=-1)


def lateral_apply(band, padded):
    return jnp.einsum("rk,pkc->prc", band, padded, precision=highest_mode)


def sheet_matrix(own_offsets, depth_psf, column_count):
    plane_rows = jnp.arange(own_offsets.shape[0], dtype=jnp.int32)[:, None]
    plane_columns = jnp.arange(column_count, dtype=jnp.int32)[None, :]
    lag_planes = plane_columns - plane_rows - own_offsets[:, None]
    depth_count = depth_psf.shape[0]
    inside = (lag_planes >= 0) & (lag_planes < depth_count)
    taps = jnp.arange(depth_count, dtype=jnp.int32)
    picked = jnp.where(lag_planes[:, :, None] == taps, depth_psf, 0.0)
    return jnp.where(inside, jnp.sum(picked, axis=-1), 0.0)


def transpose_apply(sheet_psf, values):
    return lax.dot_general(sheet_psf, values, (((0,), (0,)), ((), ())), precision=highest_mode)


def body(estimate, raw, offsets, depth_psf, lateral_psf, step_size, threshold):
    plane_count, row_count, width_count = estimate.shape
    flat_count = row_count * width_count
    halo_rows = lateral_psf.shape[0] // 2
    scan_count = lax.axis_size("scan")
    piece = flat_count // scan_count

    def to_pencil(volume):
        parts = volume.reshape(plane_count, scan_count, piece).transpose(1, 0, 2)
        return ring_exchange(parts, "scan").reshape(scan_count * plane_count, piece)

    def to_home(pencil_values):
        parts = pencil_values.reshape(scan_count, plane_count, piece)
        return ring_exchange(parts, "scan").transpose(1, 0, 2).reshape(plane_count, row_count, width_count)

    raw_pencil = to_pencil(raw)
    sheet_psf = sheet_matrix(offsets, depth_psf, offsets.shape[0])
    blur_band = band_matrix(lateral_psf, row_count, 0)
    back_band = band_matrix(lateral_psf[::-1], row_count, 0)
    padded = with_halo(estimate, "row", halo_rows)
    blurred = lateral_apply(blur_band, padded)
    pencil = to_pencil(blurred)
    predicted_pencil = jnp.dot(sheet_psf, pencil, precision=highest_mode)
    misfit_pencil = predicted_pencil - raw_pencil
    back_pencil = transpose_apply(sheet_psf, misfit_pencil)
    back_volume = to_home(back_pencil)
    back_volume, misfit_pencil = lax.optimization_barrier((back_volume, misfit_pencil))
    misfit = to_home(misfit_pencil)
    padded_back = with_halo(back_volume, "row", halo_rows)
    gradient = lateral_apply(back_band, padded_back)
    stepped = estimate - step_size[0] * gradient
    shrink_level = step_size[0] * threshold[0]
    new_estimate = jnp.sign(stepped) * jnp.maximum(jnp.abs(stepped) - shrink_level, 0.0)
    return (new_estimate, misfit)


def solution(mesh):
    placed = (P("scan", "row", None), P("scan", "row", None), P(), P(), P(), P(), P())
    return jax.shard_map(
        body,
        mesh=mesh,
        in_specs=placed,
        out_specs=(P("scan", "row", None), P("scan", "row", None)),
        check_vma=False,
    )
```

```python
import jax
import jax.numpy as jnp
from jax import lax
from jax.sharding import PartitionSpec as P

highest_mode = lax.Precision.HIGHEST


def blur_rows(band, cells, axis, width):
    count = lax.axis_size(axis)
    rows = cells.shape[1]
    summed = lateral_apply(band[:, width : width + rows], cells)
    if count == 2:
        first = lax.axis_index(axis) == 0
        sent = lax.dynamic_slice_in_dim(cells, jnp.where(first, rows - width, 0), width, axis=1)
        arrived = lax.ppermute(sent, axis, [(0, 1), (1, 0)])
        edge = jnp.where(first, band[:, width + rows :], band[:, :width])
        return summed + lateral_apply(edge, arrived)
    ends = count - 1
    head = lax.slice_in_dim(cells, 0, width, axis=1)
    tail = lax.slice_in_dim(cells, rows - width, rows, axis=1)
    above = lax.ppermute(tail, axis, [(i, (i + 1) % count) for i in range(ends)])
    below = lax.ppermute(head, axis, [((i + 1) % count, i) for i in range(ends)])
    summed = summed + lateral_apply(band[:, :width], above)
    return summed + lateral_apply(band[:, width + rows :], below)


def band_matrix(kernel_taps, row_count, shift):
    tap_count = kernel_taps.shape[0]
    out_rows = jnp.arange(row_count, dtype=jnp.int32)[:, None]
    in_rows = jnp.arange(row_count + tap_count - 1, dtype=jnp.int32)[None, :]
    lag = shift + in_rows - out_rows
    taps = jnp.arange(tap_count, dtype=jnp.int32)
    return jnp.sum(jnp.where(lag[:, :, None] == taps, kernel_taps, 0.0), axis=-1)


def lateral_apply(band, padded):
    return jnp.einsum("rk,pkc->prc", band, padded, precision=highest_mode)


def sheet_matrix(own_offsets, depth_psf, column_count):
    plane_rows = jnp.arange(own_offsets.shape[0], dtype=jnp.int32)[:, None]
    plane_columns = jnp.arange(column_count, dtype=jnp.int32)[None, :]
    lag_planes = plane_columns - plane_rows - own_offsets[:, None]
    depth_count = depth_psf.shape[0]
    inside = (lag_planes >= 0) & (lag_planes < depth_count)
    taps = jnp.arange(depth_count, dtype=jnp.int32)
    picked = jnp.where(lag_planes[:, :, None] == taps, depth_psf, 0.0)
    return jnp.where(inside, jnp.sum(picked, axis=-1), 0.0)


def transpose_apply(sheet_psf, values):
    return lax.dot_general(sheet_psf, values, (((0,), (0,)), ((), ())), precision=highest_mode)


def body(estimate, raw, offsets, depth_psf, lateral_psf, step_size, threshold):
    plane_count, row_count, width_count = estimate.shape
    flat_count = row_count * width_count
    halo_rows = lateral_psf.shape[0] // 2
    sheet_psf = sheet_matrix(offsets, depth_psf, offsets.shape[0])
    blur_band = band_matrix(lateral_psf, row_count, 0)
    back_band = band_matrix(lateral_psf[::-1], row_count, 0)
    blurred = blur_rows(blur_band, estimate, "row", halo_rows).reshape(plane_count, flat_count)
    both_flat = jnp.concatenate([blurred, raw.reshape(plane_count, flat_count)], axis=0)
    both_in = lax.all_to_all(both_flat, "scan", split_axis=1, concat_axis=0, tiled=True)
    both_in = both_in.reshape(lax.axis_size("scan"), 2, plane_count, -1)
    pencil = both_in[:, 0].reshape(offsets.shape[0], -1)
    raw_pencil = both_in[:, 1].reshape(offsets.shape[0], -1)
    predicted_pencil = jnp.dot(sheet_psf, pencil, precision=highest_mode)
    misfit_pencil = predicted_pencil - raw_pencil
    back_pencil = transpose_apply(sheet_psf, misfit_pencil)
    both_out = lax.all_to_all(jnp.stack([misfit_pencil, back_pencil]), "scan", split_axis=1, concat_axis=2, tiled=True)
    misfit = both_out[0]
    back_volume = both_out[1].reshape(plane_count, row_count, width_count)
    gradient = blur_rows(back_band, back_volume, "row", halo_rows)
    stepped = estimate - step_size[0] * gradient
    shrink_level = step_size[0] * threshold[0]
    new_estimate = jnp.sign(stepped) * jnp.maximum(jnp.abs(stepped) - shrink_level, 0.0)
    return (new_estimate, misfit.reshape(plane_count, row_count, width_count))


def solution(mesh):
    placed = (P("scan", "row", None), P("scan", "row", None), P(), P(), P(), P(), P())
    return jax.shard_map(
        body,
        mesh=mesh,
        in_specs=placed,
        out_specs=(P("scan", "row", None), P("scan", "row", None)),
        check_vma=False,
    )
```

```python
import jax
import jax.numpy as jnp
from jax import lax
from jax.sharding import PartitionSpec as P

highest_mode = lax.Precision.HIGHEST


def blur_rows(band, cells, axis, width):
    count = lax.axis_size(axis)
    rows = cells.shape[1]
    summed = lateral_apply(band[:, width : width + rows], cells)
    if count == 2:
        first = lax.axis_index(axis) == 0
        sent = lax.dynamic_slice_in_dim(cells, jnp.where(first, rows - width, 0), width, axis=1)
        arrived = lax.ppermute(sent, axis, [(0, 1), (1, 0)])
        edge = jnp.where(first, band[:, width + rows :], band[:, :width])
        return summed + lateral_apply(edge, arrived)
    ends = count - 1
    head = lax.slice_in_dim(cells, 0, width, axis=1)
    tail = lax.slice_in_dim(cells, rows - width, rows, axis=1)
    above = lax.ppermute(tail, axis, [(i, (i + 1) % count) for i in range(ends)])
    below = lax.ppermute(head, axis, [((i + 1) % count, i) for i in range(ends)])
    summed = summed + lateral_apply(band[:, :width], above)
    return summed + lateral_apply(band[:, width + rows :], below)


def band_matrix(kernel_taps, row_count, shift):
    tap_count = kernel_taps.shape[0]
    out_rows = jnp.arange(row_count, dtype=jnp.int32)[:, None]
    in_rows = jnp.arange(row_count + tap_count - 1, dtype=jnp.int32)[None, :]
    lag = shift + in_rows - out_rows
    taps = jnp.arange(tap_count, dtype=jnp.int32)
    return jnp.sum(jnp.where(lag[:, :, None] == taps, kernel_taps, 0.0), axis=-1)


def lateral_apply(band, padded):
    return jnp.einsum("rk,pkc->prc", band, padded, precision=highest_mode)


def sheet_matrix(own_offsets, depth_psf, column_count):
    plane_rows = jnp.arange(own_offsets.shape[0], dtype=jnp.int32)[:, None]
    plane_columns = jnp.arange(column_count, dtype=jnp.int32)[None, :]
    lag_planes = plane_columns - plane_rows - own_offsets[:, None]
    depth_count = depth_psf.shape[0]
    inside = (lag_planes >= 0) & (lag_planes < depth_count)
    taps = jnp.arange(depth_count, dtype=jnp.int32)
    picked = jnp.where(lag_planes[:, :, None] == taps, depth_psf, 0.0)
    return jnp.where(inside, jnp.sum(picked, axis=-1), 0.0)


def transpose_apply(sheet_psf, values):
    return lax.dot_general(sheet_psf, values, (((0,), (0,)), ((), ())), precision=highest_mode)


def body(estimate, raw, offsets, depth_psf, lateral_psf, step_size, threshold):
    plane_count, row_count, width_count = estimate.shape
    flat_count = row_count * width_count
    halo_rows = lateral_psf.shape[0] // 2
    sheet_psf = sheet_matrix(offsets, depth_psf, offsets.shape[0])
    raw_pencil = lax.all_to_all(raw.reshape(plane_count, flat_count), "scan", split_axis=1, concat_axis=0, tiled=True)
    blur_band = band_matrix(lateral_psf, row_count, 0)
    back_band = band_matrix(lateral_psf[::-1], row_count, 0)
    blurred = blur_rows(blur_band, estimate, "row", halo_rows).reshape(plane_count, flat_count)
    pencil = lax.all_to_all(blurred, "scan", split_axis=1, concat_axis=0, tiled=True)
    predicted_pencil = jnp.dot(sheet_psf, pencil, precision=highest_mode)
    misfit_pencil = predicted_pencil - raw_pencil
    back_pencil = transpose_apply(sheet_psf, misfit_pencil)
    back_flat = lax.all_to_all(back_pencil, "scan", split_axis=0, concat_axis=1, tiled=True)
    back_flat, misfit_pencil = lax.optimization_barrier((back_flat, misfit_pencil))
    misfit = lax.all_to_all(misfit_pencil, "scan", split_axis=0, concat_axis=1, tiled=True)
    back_volume = back_flat.reshape(plane_count, row_count, width_count)
    gradient = blur_rows(back_band, back_volume, "row", halo_rows)
    stepped = estimate - step_size[0] * gradient
    shrink_level = step_size[0] * threshold[0]
    new_estimate = jnp.sign(stepped) * jnp.maximum(jnp.abs(stepped) - shrink_level, 0.0)
    return (new_estimate, misfit.reshape(plane_count, row_count, width_count))


def solution(mesh):
    placed = (P("scan", "row", None), P("scan", "row", None), P(), P(), P(), P(), P())
    return jax.shard_map(
        body,
        mesh=mesh,
        in_specs=placed,
        out_specs=(P("scan", "row", None), P("scan", "row", None)),
        check_vma=False,
    )
```

```python
import jax
import jax.numpy as jnp
from jax import lax
from jax.sharding import PartitionSpec as P

highest_mode = lax.Precision.HIGHEST


def blur_rows(band, cells, axis, width):
    count = lax.axis_size(axis)
    rows = cells.shape[1]
    summed = lateral_apply(band[:, width : width + rows], cells)
    if count == 2:
        first = lax.axis_index(axis) == 0
        sent = lax.dynamic_slice_in_dim(cells, jnp.where(first, rows - width, 0), width, axis=1)
        arrived = lax.ppermute(sent, axis, [(0, 1), (1, 0)])
        edge = jnp.where(first, band[:, width + rows :], band[:, :width])
        return summed + lateral_apply(edge, arrived)
    ends = count - 1
    head = lax.slice_in_dim(cells, 0, width, axis=1)
    tail = lax.slice_in_dim(cells, rows - width, rows, axis=1)
    above = lax.ppermute(tail, axis, [(i, (i + 1) % count) for i in range(ends)])
    below = lax.ppermute(head, axis, [((i + 1) % count, i) for i in range(ends)])
    summed = summed + lateral_apply(band[:, :width], above)
    return summed + lateral_apply(band[:, width + rows :], below)


def band_matrix(kernel_taps, row_count, shift):
    tap_count = kernel_taps.shape[0]
    out_rows = jnp.arange(row_count, dtype=jnp.int32)[:, None]
    in_rows = jnp.arange(row_count + tap_count - 1, dtype=jnp.int32)[None, :]
    lag = shift + in_rows - out_rows
    taps = jnp.arange(tap_count, dtype=jnp.int32)
    return jnp.sum(jnp.where(lag[:, :, None] == taps, kernel_taps, 0.0), axis=-1)


def lateral_apply(band, padded):
    return jnp.einsum("rk,pkc->prc", band, padded, precision=highest_mode)


def sheet_matrix(own_offsets, depth_psf, column_count):
    plane_rows = jnp.arange(own_offsets.shape[0], dtype=jnp.int32)[:, None]
    plane_columns = jnp.arange(column_count, dtype=jnp.int32)[None, :]
    lag_planes = plane_columns - plane_rows - own_offsets[:, None]
    depth_count = depth_psf.shape[0]
    inside = (lag_planes >= 0) & (lag_planes < depth_count)
    taps = jnp.arange(depth_count, dtype=jnp.int32)
    picked = jnp.where(lag_planes[:, :, None] == taps, depth_psf, 0.0)
    return jnp.where(inside, jnp.sum(picked, axis=-1), 0.0)


def transpose_apply(sheet_psf, values):
    return lax.dot_general(sheet_psf, values, (((0,), (0,)), ((), ())), precision=highest_mode)


def body(estimate, raw, offsets, depth_psf, lateral_psf, step_size, threshold):
    plane_count, row_count, width_count = estimate.shape
    flat_count = row_count * width_count
    halo_rows = lateral_psf.shape[0] // 2
    sheet_psf = sheet_matrix(offsets, depth_psf, offsets.shape[0])
    blur_band = band_matrix(lateral_psf, row_count, 0)
    back_band = band_matrix(lateral_psf[::-1], row_count, 0)
    blurred = blur_rows(blur_band, estimate, "row", halo_rows).reshape(plane_count, flat_count)
    both_flat = jnp.concatenate([blurred, raw.reshape(plane_count, flat_count)], axis=0)
    both_in = lax.all_to_all(both_flat, "scan", split_axis=1, concat_axis=0, tiled=True)
    both_in = both_in.reshape(lax.axis_size("scan"), 2, plane_count, -1)
    pencil = both_in[:, 0].reshape(offsets.shape[0], -1)
    raw_pencil = both_in[:, 1].reshape(offsets.shape[0], -1)
    predicted_pencil = jnp.dot(sheet_psf, pencil, precision=highest_mode)
    misfit_pencil = predicted_pencil - raw_pencil
    back_pencil = transpose_apply(sheet_psf, misfit_pencil)
    back_flat = lax.all_to_all(back_pencil, "scan", split_axis=0, concat_axis=1, tiled=True)
    back_flat, misfit_pencil = lax.optimization_barrier((back_flat, misfit_pencil))
    misfit = lax.all_to_all(misfit_pencil, "scan", split_axis=0, concat_axis=1, tiled=True)
    back_volume = back_flat.reshape(plane_count, row_count, width_count)
    gradient = blur_rows(back_band, back_volume, "row", halo_rows)
    stepped = estimate - step_size[0] * gradient
    shrink_level = step_size[0] * threshold[0]
    new_estimate = jnp.sign(stepped) * jnp.maximum(jnp.abs(stepped) - shrink_level, 0.0)
    return (new_estimate, misfit.reshape(plane_count, row_count, width_count))


def solution(mesh):
    placed = (P("scan", "row", None), P("scan", "row", None), P(), P(), P(), P(), P())
    return jax.shard_map(
        body,
        mesh=mesh,
        in_specs=placed,
        out_specs=(P("scan", "row", None), P("scan", "row", None)),
        check_vma=False,
    )
```

```python
import jax
import jax.numpy as jnp
from jax import lax
from jax.sharding import PartitionSpec as P

highest_mode = lax.Precision.HIGHEST


def blur_rows(band, cells, axis, width):
    count = lax.axis_size(axis)
    rows = cells.shape[1]
    summed = lateral_apply(band[:, width : width + rows], cells)
    if count == 2:
        first = lax.axis_index(axis) == 0
        sent = lax.dynamic_slice_in_dim(cells, jnp.where(first, rows - width, 0), width, axis=1)
        arrived = lax.ppermute(sent, axis, [(0, 1), (1, 0)])
        edge = jnp.where(first, band[:, width + rows :], band[:, :width])
        return summed + lateral_apply(edge, arrived)
    ends = count - 1
    head = lax.slice_in_dim(cells, 0, width, axis=1)
    tail = lax.slice_in_dim(cells, rows - width, rows, axis=1)
    above = lax.ppermute(tail, axis, [(i, (i + 1) % count) for i in range(ends)])
    below = lax.ppermute(head, axis, [((i + 1) % count, i) for i in range(ends)])
    summed = summed + lateral_apply(band[:, :width], above)
    return summed + lateral_apply(band[:, width + rows :], below)


def band_matrix(kernel_taps, row_count, flip):
    tap_count = kernel_taps.shape[0]
    out_rows = jnp.arange(row_count, dtype=jnp.int32)[:, None]
    in_rows = jnp.arange(row_count + tap_count - 1, dtype=jnp.int32)[None, :]
    lag = in_rows - out_rows
    if flip:
        lag = (tap_count - 1) - lag
    taps = jnp.arange(tap_count, dtype=jnp.int32)
    return jnp.sum(jnp.where(lag[:, :, None] == taps, kernel_taps, 0.0), axis=-1)


def lateral_apply(band, padded):
    return jnp.einsum("rk,pkc->prc", band, padded, precision=highest_mode)


def sheet_matrix(own_offsets, depth_psf, column_count):
    plane_rows = jnp.arange(own_offsets.shape[0], dtype=jnp.int32)[:, None]
    plane_columns = jnp.arange(column_count, dtype=jnp.int32)[None, :]
    lag_planes = plane_columns - plane_rows - own_offsets[:, None]
    depth_count = depth_psf.shape[0]
    inside = (lag_planes >= 0) & (lag_planes < depth_count)
    taps = jnp.arange(depth_count, dtype=jnp.int32)
    picked = jnp.where(lag_planes[:, :, None] == taps, depth_psf, 0.0)
    return jnp.where(inside, jnp.sum(picked, axis=-1), 0.0)


def transpose_apply(sheet_psf, values):
    return lax.dot_general(sheet_psf, values, (((0,), (0,)), ((), ())), precision=highest_mode)


def body(estimate, raw, offsets, depth_psf, lateral_psf, step_size, threshold):
    plane_count, row_count, width_count = estimate.shape
    flat_count = row_count * width_count
    halo_rows = lateral_psf.shape[0] // 2
    sheet_psf = sheet_matrix(offsets, depth_psf, offsets.shape[0])
    blur_band = band_matrix(lateral_psf, row_count, False)
    back_band = band_matrix(lateral_psf, row_count, True)
    blurred = blur_rows(blur_band, estimate, "row", halo_rows).reshape(plane_count, flat_count)
    both_flat = jnp.concatenate([blurred, raw.reshape(plane_count, flat_count)], axis=0)
    both_in = lax.all_to_all(both_flat, "scan", split_axis=1, concat_axis=0, tiled=True)
    both_in = both_in.reshape(lax.axis_size("scan"), 2, plane_count, -1)
    pencil = both_in[:, 0].reshape(offsets.shape[0], -1)
    raw_pencil = both_in[:, 1].reshape(offsets.shape[0], -1)
    predicted_pencil = jnp.dot(sheet_psf, pencil, precision=highest_mode)
    misfit_pencil = predicted_pencil - raw_pencil
    back_pencil = transpose_apply(sheet_psf, misfit_pencil)
    both_out = lax.all_to_all(jnp.stack([misfit_pencil, back_pencil], axis=1), "scan", split_axis=0, concat_axis=2, tiled=True)
    misfit = both_out[:, 0]
    back_volume = both_out[:, 1].reshape(plane_count, row_count, width_count)
    gradient = blur_rows(back_band, back_volume, "row", halo_rows)
    stepped = estimate - step_size[0] * gradient
    shrink_level = step_size[0] * threshold[0]
    new_estimate = jnp.sign(stepped) * jnp.maximum(jnp.abs(stepped) - shrink_level, 0.0)
    return (new_estimate, misfit.reshape(plane_count, row_count, width_count))


def solution(mesh):
    placed = (P("scan", "row", None), P("scan", "row", None), P(), P(), P(), P(), P())
    return jax.shard_map(
        body,
        mesh=mesh,
        in_specs=placed,
        out_specs=(P("scan", "row", None), P("scan", "row", None)),
        check_vma=False,
    )
```

```python
import jax
import jax.numpy as jnp
from jax import lax
from jax.sharding import PartitionSpec as P

highest_mode = lax.Precision.HIGHEST


def blur_rows(band, cells, axis, width):
    count = lax.axis_size(axis)
    rows = cells.shape[1]
    summed = lateral_apply(band[:, width : width + rows], cells)
    if count == 2:
        first = lax.axis_index(axis) == 0
        sent = lax.dynamic_slice_in_dim(cells, jnp.where(first, rows - width, 0), width, axis=1)
        arrived = lax.ppermute(sent, axis, [(0, 1), (1, 0)])
        edge = jnp.where(first, band[:, width + rows :], band[:, :width])
        return summed + lateral_apply(edge, arrived)
    ends = count - 1
    head = lax.slice_in_dim(cells, 0, width, axis=1)
    tail = lax.slice_in_dim(cells, rows - width, rows, axis=1)
    above = lax.ppermute(tail, axis, [(i, (i + 1) % count) for i in range(ends)])
    below = lax.ppermute(head, axis, [((i + 1) % count, i) for i in range(ends)])
    summed = summed + lateral_apply(band[:, :width], above)
    return summed + lateral_apply(band[:, width + rows :], below)


def band_matrix(kernel_taps, row_count, flip):
    tap_count = kernel_taps.shape[0]
    out_rows = jnp.arange(row_count, dtype=jnp.int32)[:, None]
    in_rows = jnp.arange(row_count + tap_count - 1, dtype=jnp.int32)[None, :]
    lag = in_rows - out_rows
    if flip:
        lag = (tap_count - 1) - lag
    taps = jnp.arange(tap_count, dtype=jnp.int32)
    return jnp.sum(jnp.where(lag[:, :, None] == taps, kernel_taps, 0.0), axis=-1)


def lateral_apply(band, padded):
    return jnp.einsum("rk,pkc->prc", band, padded, precision=highest_mode)


def sheet_matrix(own_offsets, depth_psf, column_count):
    plane_rows = jnp.arange(own_offsets.shape[0], dtype=jnp.int32)[:, None]
    plane_columns = jnp.arange(column_count, dtype=jnp.int32)[None, :]
    lag_planes = plane_columns - plane_rows - own_offsets[:, None]
    depth_count = depth_psf.shape[0]
    inside = (lag_planes >= 0) & (lag_planes < depth_count)
    taps = jnp.arange(depth_count, dtype=jnp.int32)
    picked = jnp.where(lag_planes[:, :, None] == taps, depth_psf, 0.0)
    return jnp.where(inside, jnp.sum(picked, axis=-1), 0.0)


def transpose_apply(sheet_psf, values):
    return lax.dot_general(sheet_psf, values, (((0,), (0,)), ((), ())), precision=highest_mode)


def body(estimate, raw, offsets, depth_psf, lateral_psf, step_size, threshold):
    plane_count, row_count, width_count = estimate.shape
    flat_count = row_count * width_count
    halo_rows = lateral_psf.shape[0] // 2
    sheet_psf = sheet_matrix(offsets, depth_psf, offsets.shape[0])
    blur_band = band_matrix(lateral_psf, row_count, False)
    back_band = band_matrix(lateral_psf, row_count, True)
    blurred = blur_rows(blur_band, estimate, "row", halo_rows).reshape(plane_count, flat_count)
    both_flat = jnp.concatenate([blurred, raw.reshape(plane_count, flat_count)], axis=0)
    both_in = lax.all_to_all(both_flat, "scan", split_axis=1, concat_axis=0, tiled=True)
    both_in = both_in.reshape(lax.axis_size("scan"), 2, plane_count, -1)
    pencil = both_in[:, 0].reshape(offsets.shape[0], -1)
    raw_pencil = both_in[:, 1].reshape(offsets.shape[0], -1)
    predicted_pencil = jnp.dot(sheet_psf, pencil, precision=highest_mode)
    misfit_pencil = predicted_pencil - raw_pencil
    scan_count = lax.axis_size("scan")
    all_planes = offsets.shape[0]
    keep = jnp.eye(all_planes, dtype=jnp.float32).reshape(scan_count, 1, plane_count, all_planes)
    spread = sheet_psf.T.reshape(scan_count, 1, plane_count, all_planes)
    joint = jnp.concatenate([keep, spread], axis=1).reshape(2 * all_planes, all_planes)
    both_pencil = jnp.dot(joint, misfit_pencil, precision=highest_mode)
    both_out = lax.all_to_all(both_pencil, "scan", split_axis=0, concat_axis=1, tiled=True)
    misfit = both_out[:plane_count]
    back_volume = both_out[plane_count:].reshape(plane_count, row_count, width_count)
    gradient = blur_rows(back_band, back_volume, "row", halo_rows)
    stepped = estimate - step_size[0] * gradient
    shrink_level = step_size[0] * threshold[0]
    new_estimate = jnp.sign(stepped) * jnp.maximum(jnp.abs(stepped) - shrink_level, 0.0)
    return (new_estimate, misfit.reshape(plane_count, row_count, width_count))


def solution(mesh):
    placed = (P("scan", "row", None), P("scan", "row", None), P(), P(), P(), P(), P())
    return jax.shard_map(
        body,
        mesh=mesh,
        in_specs=placed,
        out_specs=(P("scan", "row", None), P("scan", "row", None)),
        check_vma=False,
    )
```

```python
import jax
import jax.numpy as jnp
from jax import lax
from jax.sharding import PartitionSpec as P

highest_mode = lax.Precision.HIGHEST


def blur_rows(band, cells, axis, width):
    count = lax.axis_size(axis)
    rows = cells.shape[1]
    summed = lateral_apply(band[:, width : width + rows], cells)
    if count == 2:
        first = lax.axis_index(axis) == 0
        sent = lax.dynamic_slice_in_dim(cells, jnp.where(first, rows - width, 0), width, axis=1)
        arrived = lax.ppermute(sent, axis, [(0, 1), (1, 0)])
        edge = jnp.where(first, band[:, width + rows :], band[:, :width])
        return summed + lateral_apply(edge, arrived)
    ends = count - 1
    head = lax.slice_in_dim(cells, 0, width, axis=1)
    tail = lax.slice_in_dim(cells, rows - width, rows, axis=1)
    above = lax.ppermute(tail, axis, [(i, (i + 1) % count) for i in range(ends)])
    below = lax.ppermute(head, axis, [((i + 1) % count, i) for i in range(ends)])
    summed = summed + lateral_apply(band[:, :width], above)
    return summed + lateral_apply(band[:, width + rows :], below)


def band_matrix(kernel_taps, row_count, flip):
    tap_count = kernel_taps.shape[0]
    out_rows = jnp.arange(row_count, dtype=jnp.int32)[:, None]
    in_rows = jnp.arange(row_count + tap_count - 1, dtype=jnp.int32)[None, :]
    lag = in_rows - out_rows
    if flip:
        lag = (tap_count - 1) - lag
    taps = jnp.arange(tap_count, dtype=jnp.int32)
    return jnp.sum(jnp.where(lag[:, :, None] == taps, kernel_taps, 0.0), axis=-1)


def lateral_apply(band, padded):
    return jnp.einsum("rk,pkc->prc", band, padded, precision=highest_mode)


def sheet_matrix(own_offsets, depth_psf, column_count):
    plane_rows = jnp.arange(own_offsets.shape[0], dtype=jnp.int32)[:, None]
    plane_columns = jnp.arange(column_count, dtype=jnp.int32)[None, :]
    lag_planes = plane_columns - plane_rows - own_offsets[:, None]
    depth_count = depth_psf.shape[0]
    inside = (lag_planes >= 0) & (lag_planes < depth_count)
    taps = jnp.arange(depth_count, dtype=jnp.int32)
    picked = jnp.where(lag_planes[:, :, None] == taps, depth_psf, 0.0)
    return jnp.where(inside, jnp.sum(picked, axis=-1), 0.0)


def transpose_apply(sheet_psf, values):
    return lax.dot_general(sheet_psf, values, (((0,), (0,)), ((), ())), precision=highest_mode)


def body(estimate, raw, offsets, depth_psf, lateral_psf, step_size, threshold):
    plane_count, row_count, width_count = estimate.shape
    flat_count = row_count * width_count
    halo_rows = lateral_psf.shape[0] // 2
    sheet_psf = sheet_matrix(offsets, depth_psf, offsets.shape[0])
    blur_band = band_matrix(lateral_psf, row_count, False)
    back_band = band_matrix(lateral_psf, row_count, True)
    chunk_count = lax.axis_size("scan")
    raw_chunks = raw.reshape(plane_count, chunk_count, flat_count // chunk_count).transpose(1, 0, 2)
    blurred = blur_rows(blur_band, estimate, "row", halo_rows)
    blurred_chunks = blurred.reshape(plane_count, chunk_count, flat_count // chunk_count).transpose(1, 0, 2)
    both_chunks = jnp.concatenate([blurred_chunks, raw_chunks], axis=1)
    both_in = lax.all_to_all(both_chunks, "scan", split_axis=0, concat_axis=0, tiled=True)
    pencil = both_in[:, :plane_count].reshape(offsets.shape[0], -1)
    raw_pencil = both_in[:, plane_count:].reshape(offsets.shape[0], -1)
    predicted_pencil = jnp.dot(sheet_psf, pencil, precision=highest_mode)
    misfit_pencil = predicted_pencil - raw_pencil
    scan_count = lax.axis_size("scan")
    all_planes = offsets.shape[0]
    keep = jnp.eye(all_planes, dtype=jnp.float32).reshape(scan_count, 1, plane_count, all_planes)
    spread = sheet_psf.T.reshape(scan_count, 1, plane_count, all_planes)
    joint = jnp.concatenate([keep, spread], axis=1).reshape(2 * all_planes, all_planes)
    both_pencil = jnp.dot(joint, misfit_pencil, precision=highest_mode)
    both_out = lax.all_to_all(both_pencil, "scan", split_axis=0, concat_axis=1, tiled=True)
    misfit = both_out[:plane_count]
    back_volume = both_out[plane_count:].reshape(plane_count, row_count, width_count)
    gradient = blur_rows(back_band, back_volume, "row", halo_rows)
    stepped = estimate - step_size[0] * gradient
    shrink_level = step_size[0] * threshold[0]
    new_estimate = jnp.sign(stepped) * jnp.maximum(jnp.abs(stepped) - shrink_level, 0.0)
    return (new_estimate, misfit.reshape(plane_count, row_count, width_count))


def solution(mesh):
    placed = (P("scan", "row", None), P("scan", "row", None), P(), P(), P(), P(), P())
    return jax.shard_map(
        body,
        mesh=mesh,
        in_specs=placed,
        out_specs=(P("scan", "row", None), P("scan", "row", None)),
        check_vma=False,
    )
```

```python
import jax
import jax.numpy as jnp
from jax import lax
from jax.sharding import PartitionSpec as P

matmul_mode = lax.Precision.HIGH


def blur_rows(band, cells, axis, width):
    count = lax.axis_size(axis)
    rows = cells.shape[1]
    summed = lateral_apply(band[:, width : width + rows], cells)
    if count == 2:
        first = lax.axis_index(axis) == 0
        sent = lax.dynamic_slice_in_dim(cells, jnp.where(first, rows - width, 0), width, axis=1)
        arrived = lax.ppermute(sent, axis, [(0, 1), (1, 0)])
        edge = jnp.where(first, band[:, width + rows :], band[:, :width])
        return summed + lateral_apply(edge, arrived)
    ends = count - 1
    head = lax.slice_in_dim(cells, 0, width, axis=1)
    tail = lax.slice_in_dim(cells, rows - width, rows, axis=1)
    above = lax.ppermute(tail, axis, [(i, (i + 1) % count) for i in range(ends)])
    below = lax.ppermute(head, axis, [((i + 1) % count, i) for i in range(ends)])
    summed = summed + lateral_apply(band[:, :width], above)
    return summed + lateral_apply(band[:, width + rows :], below)


def band_matrix(kernel_taps, row_count, flip):
    tap_count = kernel_taps.shape[0]
    out_rows = jnp.arange(row_count, dtype=jnp.int32)[:, None]
    in_rows = jnp.arange(row_count + tap_count - 1, dtype=jnp.int32)[None, :]
    lag = in_rows - out_rows
    if flip:
        lag = (tap_count - 1) - lag
    taps = jnp.arange(tap_count, dtype=jnp.int32)
    return jnp.sum(jnp.where(lag[:, :, None] == taps, kernel_taps, 0.0), axis=-1)


def lateral_apply(band, padded):
    return jnp.einsum("rk,pkc->prc", band, padded, precision=matmul_mode)


def sheet_matrix(own_offsets, depth_psf, column_count):
    plane_rows = jnp.arange(own_offsets.shape[0], dtype=jnp.int32)[:, None]
    plane_columns = jnp.arange(column_count, dtype=jnp.int32)[None, :]
    lag_planes = plane_columns - plane_rows - own_offsets[:, None]
    depth_count = depth_psf.shape[0]
    inside = (lag_planes >= 0) & (lag_planes < depth_count)
    taps = jnp.arange(depth_count, dtype=jnp.int32)
    picked = jnp.where(lag_planes[:, :, None] == taps, depth_psf, 0.0)
    return jnp.where(inside, jnp.sum(picked, axis=-1), 0.0)


def transpose_apply(sheet_psf, values):
    return lax.dot_general(sheet_psf, values, (((0,), (0,)), ((), ())), precision=matmul_mode)


def body(estimate, raw, offsets, depth_psf, lateral_psf, step_size, threshold):
    plane_count, row_count, width_count = estimate.shape
    flat_count = row_count * width_count
    halo_rows = lateral_psf.shape[0] // 2
    sheet_psf = sheet_matrix(offsets, depth_psf, offsets.shape[0])
    blur_band = band_matrix(lateral_psf, row_count, False)
    back_band = band_matrix(lateral_psf, row_count, True)
    blurred = blur_rows(blur_band, estimate, "row", halo_rows).reshape(plane_count, flat_count)
    both_flat = jnp.concatenate([blurred, raw.reshape(plane_count, flat_count)], axis=0)
    both_in = lax.all_to_all(both_flat, "scan", split_axis=1, concat_axis=0, tiled=True)
    both_in = both_in.reshape(lax.axis_size("scan"), 2, plane_count, -1)
    pencil = both_in[:, 0].reshape(offsets.shape[0], -1)
    raw_pencil = both_in[:, 1].reshape(offsets.shape[0], -1)
    predicted_pencil = jnp.dot(sheet_psf, pencil, precision=matmul_mode)
    misfit_pencil = predicted_pencil - raw_pencil
    scan_count = lax.axis_size("scan")
    all_planes = offsets.shape[0]
    keep = jnp.eye(all_planes, dtype=jnp.float32).reshape(scan_count, 1, plane_count, all_planes)
    spread = sheet_psf.T.reshape(scan_count, 1, plane_count, all_planes)
    joint = jnp.concatenate([keep, spread], axis=1).reshape(2 * all_planes, all_planes)
    both_pencil = jnp.dot(joint, misfit_pencil, precision=matmul_mode)
    both_out = lax.all_to_all(both_pencil, "scan", split_axis=0, concat_axis=1, tiled=True)
    misfit = both_out[:plane_count]
    back_volume = both_out[plane_count:].reshape(plane_count, row_count, width_count)
    gradient = blur_rows(back_band, back_volume, "row", halo_rows)
    stepped = estimate - step_size[0] * gradient
    shrink_level = step_size[0] * threshold[0]
    new_estimate = jnp.sign(stepped) * jnp.maximum(jnp.abs(stepped) - shrink_level, 0.0)
    return (new_estimate, misfit.reshape(plane_count, row_count, width_count))


def solution(mesh):
    placed = (P("scan", "row", None), P("scan", "row", None), P(), P(), P(), P(), P())
    return jax.shard_map(
        body,
        mesh=mesh,
        in_specs=placed,
        out_specs=(P("scan", "row", None), P("scan", "row", None)),
        check_vma=False,
    )
```

```python
import jax
import jax.numpy as jnp
from jax import lax
from jax.sharding import PartitionSpec as P

highest_mode = lax.Precision.HIGHEST
high_mode = lax.Precision.HIGH


def blur_rows(band, cells, axis, width, precision=highest_mode):
    count = lax.axis_size(axis)
    rows = cells.shape[1]
    summed = lateral_apply(band[:, width : width + rows], cells, precision)
    if count == 2:
        first = lax.axis_index(axis) == 0
        sent = lax.dynamic_slice_in_dim(cells, jnp.where(first, rows - width, 0), width, axis=1)
        arrived = lax.ppermute(sent, axis, [(0, 1), (1, 0)])
        edge = jnp.where(first, band[:, width + rows :], band[:, :width])
        return summed + lateral_apply(edge, arrived, precision)
    ends = count - 1
    head = lax.slice_in_dim(cells, 0, width, axis=1)
    tail = lax.slice_in_dim(cells, rows - width, rows, axis=1)
    above = lax.ppermute(tail, axis, [(i, (i + 1) % count) for i in range(ends)])
    below = lax.ppermute(head, axis, [((i + 1) % count, i) for i in range(ends)])
    summed = summed + lateral_apply(band[:, :width], above, precision)
    return summed + lateral_apply(band[:, width + rows :], below, precision)


def band_matrix(kernel_taps, row_count, flip):
    tap_count = kernel_taps.shape[0]
    out_rows = jnp.arange(row_count, dtype=jnp.int32)[:, None]
    in_rows = jnp.arange(row_count + tap_count - 1, dtype=jnp.int32)[None, :]
    lag = in_rows - out_rows
    if flip:
        lag = (tap_count - 1) - lag
    taps = jnp.arange(tap_count, dtype=jnp.int32)
    return jnp.sum(jnp.where(lag[:, :, None] == taps, kernel_taps, 0.0), axis=-1)


def lateral_apply(band, padded, precision=highest_mode):
    return jnp.einsum("rk,pkc->prc", band, padded, precision=precision)


def sheet_matrix(own_offsets, depth_psf, column_count):
    plane_rows = jnp.arange(own_offsets.shape[0], dtype=jnp.int32)[:, None]
    plane_columns = jnp.arange(column_count, dtype=jnp.int32)[None, :]
    lag_planes = plane_columns - plane_rows - own_offsets[:, None]
    depth_count = depth_psf.shape[0]
    inside = (lag_planes >= 0) & (lag_planes < depth_count)
    taps = jnp.arange(depth_count, dtype=jnp.int32)
    picked = jnp.where(lag_planes[:, :, None] == taps, depth_psf, 0.0)
    return jnp.where(inside, jnp.sum(picked, axis=-1), 0.0)


def transpose_apply(sheet_psf, values):
    return lax.dot_general(sheet_psf, values, (((0,), (0,)), ((), ())), precision=highest_mode)


def body(estimate, raw, offsets, depth_psf, lateral_psf, step_size, threshold):
    plane_count, row_count, width_count = estimate.shape
    flat_count = row_count * width_count
    halo_rows = lateral_psf.shape[0] // 2
    sheet_psf = sheet_matrix(offsets, depth_psf, offsets.shape[0])
    blur_band = band_matrix(lateral_psf, row_count, False)
    back_band = band_matrix(lateral_psf, row_count, True)
    blurred = blur_rows(blur_band, estimate, "row", halo_rows).reshape(plane_count, flat_count)
    both_flat = jnp.concatenate([blurred, raw.reshape(plane_count, flat_count)], axis=0)
    both_in = lax.all_to_all(both_flat, "scan", split_axis=1, concat_axis=0, tiled=True)
    both_in = both_in.reshape(lax.axis_size("scan"), 2, plane_count, -1)
    pencil = both_in[:, 0].reshape(offsets.shape[0], -1)
    raw_pencil = both_in[:, 1].reshape(offsets.shape[0], -1)
    predicted_pencil = jnp.dot(sheet_psf, pencil, precision=highest_mode)
    misfit_pencil = predicted_pencil - raw_pencil
    scan_count = lax.axis_size("scan")
    all_planes = offsets.shape[0]
    keep = jnp.eye(all_planes, dtype=jnp.float32).reshape(scan_count, 1, plane_count, all_planes)
    spread = sheet_psf.T.reshape(scan_count, 1, plane_count, all_planes)
    joint = jnp.concatenate([keep, spread], axis=1).reshape(2 * all_planes, all_planes)
    both_pencil = jnp.dot(joint, misfit_pencil, precision=high_mode)
    both_out = lax.all_to_all(both_pencil, "scan", split_axis=0, concat_axis=1, tiled=True)
    misfit = both_out[:plane_count]
    back_volume = both_out[plane_count:].reshape(plane_count, row_count, width_count)
    gradient = blur_rows(back_band, back_volume, "row", halo_rows, high_mode)
    stepped = estimate - step_size[0] * gradient
    shrink_level = step_size[0] * threshold[0]
    new_estimate = jnp.sign(stepped) * jnp.maximum(jnp.abs(stepped) - shrink_level, 0.0)
    return (new_estimate, misfit.reshape(plane_count, row_count, width_count))


def solution(mesh):
    placed = (P("scan", "row", None), P("scan", "row", None), P(), P(), P(), P(), P())
    return jax.shard_map(
        body,
        mesh=mesh,
        in_specs=placed,
        out_specs=(P("scan", "row", None), P("scan", "row", None)),
        check_vma=False,
    )
```

```python
import jax
import jax.numpy as jnp
from jax import lax
from jax.sharding import PartitionSpec as P

highest_mode = lax.Precision.HIGHEST


def blur_rows(band, cells, axis, width):
    count = lax.axis_size(axis)
    rows = cells.shape[1]
    summed = lateral_apply(band[:, width : width + rows], cells)
    if count == 2:
        first = lax.axis_index(axis) == 0
        sent = lax.dynamic_slice_in_dim(cells, jnp.where(first, rows - width, 0), width, axis=1)
        arrived = lax.ppermute(sent, axis, [(0, 1), (1, 0)])
        edge = jnp.where(first, band[:, width + rows :], band[:, :width])
        return summed + lateral_apply(edge, arrived)
    ends = count - 1
    head = lax.slice_in_dim(cells, 0, width, axis=1)
    tail = lax.slice_in_dim(cells, rows - width, rows, axis=1)
    above = lax.ppermute(tail, axis, [(i, (i + 1) % count) for i in range(ends)])
    below = lax.ppermute(head, axis, [((i + 1) % count, i) for i in range(ends)])
    summed = summed + lateral_apply(band[:, :width], above)
    return summed + lateral_apply(band[:, width + rows :], below)


def chunked_forward(estimate, raw, band, sheet_psf, width, chunk_count):
    plane_count, rows, columns = estimate.shape
    per_chunk = rows // chunk_count
    first = lax.axis_index("row") == 0
    sent = lax.dynamic_slice_in_dim(estimate, jnp.where(first, rows - width, 0), width, axis=1)
    arrived = lax.ppermute(sent, "row", [(0, 1), (1, 0)])
    stacked = jnp.concatenate([estimate, raw], axis=1)
    own = band[:, width : width + rows]
    keep = jnp.eye(rows, dtype=own.dtype)
    zero = jnp.zeros_like(own)
    joint = jnp.stack([jnp.concatenate([own, zero], axis=1), jnp.concatenate([zero, keep], axis=1)])
    joint = joint.reshape(2, chunk_count, per_chunk, 2 * rows).transpose(1, 0, 2, 3)
    edge = jnp.where(first, band[:, width + rows :], band[:, :width])
    edge = jnp.stack([edge, jnp.zeros_like(edge)]).reshape(2, chunk_count, per_chunk, width).transpose(1, 0, 2, 3)
    outgoing = jnp.einsum("karj,pjc->karpc", joint, stacked, precision=highest_mode)
    outgoing = outgoing + jnp.einsum("karj,pjc->karpc", edge, arrived, precision=highest_mode)
    incoming = lax.all_to_all(outgoing, "scan", split_axis=0, concat_axis=0, tiled=True)
    all_planes = sheet_psf.shape[0]
    sheet_parts = sheet_psf.reshape(all_planes, chunk_count, plane_count)
    predicted = jnp.einsum("qsp,srpc->qrc", sheet_parts, incoming[:, 0], precision=highest_mode)
    raw_pencil = incoming[:, 1].transpose(0, 2, 1, 3).reshape(all_planes, per_chunk, columns)
    return (predicted - raw_pencil).reshape(all_planes, per_chunk * columns)


def band_matrix(kernel_taps, row_count, flip):
    tap_count = kernel_taps.shape[0]
    out_rows = jnp.arange(row_count, dtype=jnp.int32)[:, None]
    in_rows = jnp.arange(row_count + tap_count - 1, dtype=jnp.int32)[None, :]
    lag = in_rows - out_rows
    if flip:
        lag = (tap_count - 1) - lag
    taps = jnp.arange(tap_count, dtype=jnp.int32)
    return jnp.sum(jnp.where(lag[:, :, None] == taps, kernel_taps, 0.0), axis=-1)


def lateral_apply(band, padded):
    return jnp.einsum("rk,pkc->prc", band, padded, precision=highest_mode)


def sheet_matrix(own_offsets, depth_psf, column_count):
    plane_rows = jnp.arange(own_offsets.shape[0], dtype=jnp.int32)[:, None]
    plane_columns = jnp.arange(column_count, dtype=jnp.int32)[None, :]
    lag_planes = plane_columns - plane_rows - own_offsets[:, None]
    depth_count = depth_psf.shape[0]
    inside = (lag_planes >= 0) & (lag_planes < depth_count)
    taps = jnp.arange(depth_count, dtype=jnp.int32)
    picked = jnp.where(lag_planes[:, :, None] == taps, depth_psf, 0.0)
    return jnp.where(inside, jnp.sum(picked, axis=-1), 0.0)


def transpose_apply(sheet_psf, values):
    return lax.dot_general(sheet_psf, values, (((0,), (0,)), ((), ())), precision=highest_mode)


def body(estimate, raw, offsets, depth_psf, lateral_psf, step_size, threshold):
    plane_count, row_count, width_count = estimate.shape
    flat_count = row_count * width_count
    halo_rows = lateral_psf.shape[0] // 2
    sheet_psf = sheet_matrix(offsets, depth_psf, offsets.shape[0])
    blur_band = band_matrix(lateral_psf, row_count, False)
    back_band = band_matrix(lateral_psf, row_count, True)
    scan_count = lax.axis_size("scan")
    if row_count % scan_count == 0 and lax.axis_size("row") == 2:
        misfit_pencil = chunked_forward(estimate, raw, blur_band, sheet_psf, halo_rows, scan_count)
    else:
        blurred = blur_rows(blur_band, estimate, "row", halo_rows).reshape(plane_count, flat_count)
        both_flat = jnp.concatenate([blurred, raw.reshape(plane_count, flat_count)], axis=0)
        both_in = lax.all_to_all(both_flat, "scan", split_axis=1, concat_axis=0, tiled=True)
        both_in = both_in.reshape(scan_count, 2, plane_count, -1)
        pencil = both_in[:, 0].reshape(offsets.shape[0], -1)
        raw_pencil = both_in[:, 1].reshape(offsets.shape[0], -1)
        predicted_pencil = jnp.dot(sheet_psf, pencil, precision=highest_mode)
        misfit_pencil = predicted_pencil - raw_pencil
    scan_count = lax.axis_size("scan")
    all_planes = offsets.shape[0]
    keep = jnp.eye(all_planes, dtype=jnp.float32).reshape(scan_count, 1, plane_count, all_planes)
    spread = sheet_psf.T.reshape(scan_count, 1, plane_count, all_planes)
    joint = jnp.concatenate([keep, spread], axis=1).reshape(2 * all_planes, all_planes)
    both_pencil = jnp.dot(joint, misfit_pencil, precision=highest_mode)
    both_out = lax.all_to_all(both_pencil, "scan", split_axis=0, concat_axis=1, tiled=True)
    misfit = both_out[:plane_count]
    back_volume = both_out[plane_count:].reshape(plane_count, row_count, width_count)
    gradient = blur_rows(back_band, back_volume, "row", halo_rows)
    stepped = estimate - step_size[0] * gradient
    shrink_level = step_size[0] * threshold[0]
    new_estimate = jnp.sign(stepped) * jnp.maximum(jnp.abs(stepped) - shrink_level, 0.0)
    return (new_estimate, misfit.reshape(plane_count, row_count, width_count))


def solution(mesh):
    placed = (P("scan", "row", None), P("scan", "row", None), P(), P(), P(), P(), P())
    return jax.shard_map(
        body,
        mesh=mesh,
        in_specs=placed,
        out_specs=(P("scan", "row", None), P("scan", "row", None)),
        check_vma=False,
    )
```

```python
import jax
import jax.numpy as jnp
from jax import lax
from jax.sharding import PartitionSpec as P

highest_mode = lax.Precision.HIGHEST
high_mode = lax.Precision.HIGH


def blur_rows(band, cells, axis, width, precision=highest_mode):
    count = lax.axis_size(axis)
    rows = cells.shape[1]
    summed = lateral_apply(band[:, width : width + rows], cells, precision)
    if count == 2:
        first = lax.axis_index(axis) == 0
        sent = lax.dynamic_slice_in_dim(cells, jnp.where(first, rows - width, 0), width, axis=1)
        arrived = lax.ppermute(sent, axis, [(0, 1), (1, 0)])
        edge = jnp.where(first, band[:, width + rows :], band[:, :width])
        return summed + lateral_apply(edge, arrived, precision)
    ends = count - 1
    head = lax.slice_in_dim(cells, 0, width, axis=1)
    tail = lax.slice_in_dim(cells, rows - width, rows, axis=1)
    above = lax.ppermute(tail, axis, [(i, (i + 1) % count) for i in range(ends)])
    below = lax.ppermute(head, axis, [((i + 1) % count, i) for i in range(ends)])
    summed = summed + lateral_apply(band[:, :width], above, precision)
    return summed + lateral_apply(band[:, width + rows :], below, precision)


def chunked_gradient(band, chunks, width):
    chunk_count, plane_count, per_chunk, columns = chunks.shape
    rows = chunk_count * per_chunk
    halo_chunks = width // per_chunk
    first = lax.axis_index("row") == 0
    own = band[:, width : width + rows].reshape(rows, chunk_count, per_chunk)
    summed = jnp.einsum("rkj,kpjc->prc", own, chunks, precision=high_mode)
    sent = lax.dynamic_slice_in_dim(chunks, jnp.where(first, chunk_count - halo_chunks, 0), halo_chunks, axis=0)
    arrived = lax.ppermute(sent, "row", [(0, 1), (1, 0)])
    edge = jnp.where(first, band[:, width + rows :], band[:, :width]).reshape(rows, halo_chunks, per_chunk)
    return summed + jnp.einsum("rkj,kpjc->prc", edge, arrived, precision=high_mode)


def band_matrix(kernel_taps, row_count, flip):
    tap_count = kernel_taps.shape[0]
    out_rows = jnp.arange(row_count, dtype=jnp.int32)[:, None]
    in_rows = jnp.arange(row_count + tap_count - 1, dtype=jnp.int32)[None, :]
    lag = in_rows - out_rows
    if flip:
        lag = (tap_count - 1) - lag
    taps = jnp.arange(tap_count, dtype=jnp.int32)
    return jnp.sum(jnp.where(lag[:, :, None] == taps, kernel_taps, 0.0), axis=-1)


def lateral_apply(band, padded, precision=highest_mode):
    return jnp.einsum("rk,pkc->prc", band, padded, precision=precision)


def sheet_matrix(own_offsets, depth_psf, column_count):
    plane_rows = jnp.arange(own_offsets.shape[0], dtype=jnp.int32)[:, None]
    plane_columns = jnp.arange(column_count, dtype=jnp.int32)[None, :]
    lag_planes = plane_columns - plane_rows - own_offsets[:, None]
    depth_count = depth_psf.shape[0]
    inside = (lag_planes >= 0) & (lag_planes < depth_count)
    taps = jnp.arange(depth_count, dtype=jnp.int32)
    picked = jnp.where(lag_planes[:, :, None] == taps, depth_psf, 0.0)
    return jnp.where(inside, jnp.sum(picked, axis=-1), 0.0)


def transpose_apply(sheet_psf, values):
    return lax.dot_general(sheet_psf, values, (((0,), (0,)), ((), ())), precision=highest_mode)


def body(estimate, raw, offsets, depth_psf, lateral_psf, step_size, threshold):
    plane_count, row_count, width_count = estimate.shape
    flat_count = row_count * width_count
    halo_rows = lateral_psf.shape[0] // 2
    sheet_psf = sheet_matrix(offsets, depth_psf, offsets.shape[0])
    blur_band = band_matrix(lateral_psf, row_count, False)
    back_band = band_matrix(lateral_psf, row_count, True)
    blurred = blur_rows(blur_band, estimate, "row", halo_rows).reshape(plane_count, flat_count)
    both_flat = jnp.concatenate([blurred, raw.reshape(plane_count, flat_count)], axis=0)
    both_in = lax.all_to_all(both_flat, "scan", split_axis=1, concat_axis=0, tiled=True)
    both_in = both_in.reshape(lax.axis_size("scan"), 2, plane_count, -1)
    pencil = both_in[:, 0].reshape(offsets.shape[0], -1)
    raw_pencil = both_in[:, 1].reshape(offsets.shape[0], -1)
    predicted_pencil = jnp.dot(sheet_psf, pencil, precision=highest_mode)
    misfit_pencil = predicted_pencil - raw_pencil
    scan_count = lax.axis_size("scan")
    all_planes = offsets.shape[0]
    keep = jnp.eye(all_planes, dtype=jnp.float32).reshape(scan_count, 1, plane_count, all_planes)
    spread = sheet_psf.T.reshape(scan_count, 1, plane_count, all_planes)
    joint = jnp.concatenate([keep, spread], axis=1).reshape(2 * all_planes, all_planes)
    both_pencil = jnp.dot(joint, misfit_pencil, precision=high_mode)
    if row_count % scan_count == 0 and lax.axis_size("row") == 2:
        per_chunk = row_count // scan_count
        incoming = lax.all_to_all(both_pencil.reshape(scan_count, 2 * plane_count, -1), "scan", split_axis=0, concat_axis=0, tiled=True)
        misfit = incoming[:, :plane_count].transpose(1, 0, 2).reshape(plane_count, flat_count)
        back_chunks = incoming[:, plane_count:].reshape(scan_count, plane_count, per_chunk, width_count)
        gradient = chunked_gradient(back_band, back_chunks, halo_rows)
    else:
        both_out = lax.all_to_all(both_pencil, "scan", split_axis=0, concat_axis=1, tiled=True)
        misfit = both_out[:plane_count]
        back_volume = both_out[plane_count:].reshape(plane_count, row_count, width_count)
        gradient = blur_rows(back_band, back_volume, "row", halo_rows, high_mode)
    stepped = estimate - step_size[0] * gradient
    shrink_level = step_size[0] * threshold[0]
    new_estimate = jnp.sign(stepped) * jnp.maximum(jnp.abs(stepped) - shrink_level, 0.0)
    return (new_estimate, misfit.reshape(plane_count, row_count, width_count))


def solution(mesh):
    placed = (P("scan", "row", None), P("scan", "row", None), P(), P(), P(), P(), P())
    return jax.shard_map(
        body,
        mesh=mesh,
        in_specs=placed,
        out_specs=(P("scan", "row", None), P("scan", "row", None)),
        check_vma=False,
    )
```

```python
import jax
import jax.numpy as jnp
from jax import lax
from jax.sharding import PartitionSpec as P

highest_mode = lax.Precision.HIGHEST
high_mode = lax.Precision.HIGH


def blur_rows(band, cells, axis, width, precision=highest_mode):
    count = lax.axis_size(axis)
    rows = cells.shape[1]
    summed = lateral_apply(band[:, width : width + rows], cells, precision)
    if count == 2:
        first = lax.axis_index(axis) == 0
        sent = lax.dynamic_slice_in_dim(cells, jnp.where(first, rows - width, 0), width, axis=1)
        arrived = lax.ppermute(sent, axis, [(0, 1), (1, 0)])
        edge = jnp.where(first, band[:, width + rows :], band[:, :width])
        return summed + lateral_apply(edge, arrived, precision)
    ends = count - 1
    head = lax.slice_in_dim(cells, 0, width, axis=1)
    tail = lax.slice_in_dim(cells, rows - width, rows, axis=1)
    above = lax.ppermute(tail, axis, [(i, (i + 1) % count) for i in range(ends)])
    below = lax.ppermute(head, axis, [((i + 1) % count, i) for i in range(ends)])
    summed = summed + lateral_apply(band[:, :width], above, precision)
    return summed + lateral_apply(band[:, width + rows :], below, precision)


def band_matrix(kernel_taps, row_count, flip):
    tap_count = kernel_taps.shape[0]
    out_rows = jnp.arange(row_count, dtype=jnp.int32)[:, None]
    in_rows = jnp.arange(row_count + tap_count - 1, dtype=jnp.int32)[None, :]
    lag = in_rows - out_rows
    if flip:
        lag = (tap_count - 1) - lag
    taps = jnp.arange(tap_count, dtype=jnp.int32)
    return jnp.sum(jnp.where(lag[:, :, None] == taps, kernel_taps, 0.0), axis=-1)


def lateral_apply(band, padded, precision=highest_mode):
    return jnp.einsum("rk,pkc->prc", band, padded, precision=precision)


def sheet_matrix(own_offsets, depth_psf, column_count):
    plane_rows = jnp.arange(own_offsets.shape[0], dtype=jnp.int32)[:, None]
    plane_columns = jnp.arange(column_count, dtype=jnp.int32)[None, :]
    lag_planes = plane_columns - plane_rows - own_offsets[:, None]
    depth_count = depth_psf.shape[0]
    inside = (lag_planes >= 0) & (lag_planes < depth_count)
    taps = jnp.arange(depth_count, dtype=jnp.int32)
    picked = jnp.where(lag_planes[:, :, None] == taps, depth_psf, 0.0)
    return jnp.where(inside, jnp.sum(picked, axis=-1), 0.0)


def transpose_apply(sheet_psf, values):
    return lax.dot_general(sheet_psf, values, (((0,), (0,)), ((), ())), precision=highest_mode)


def body(estimate, raw, offsets, depth_psf, lateral_psf, step_size, threshold):
    plane_count, row_count, width_count = estimate.shape
    flat_count = row_count * width_count
    halo_rows = lateral_psf.shape[0] // 2
    sheet_psf = sheet_matrix(offsets, depth_psf, offsets.shape[0])
    blur_band = band_matrix(lateral_psf, row_count, False)
    back_band = band_matrix(lateral_psf, row_count, True)
    blurred = blur_rows(blur_band, estimate, "row", halo_rows).reshape(plane_count, flat_count)
    both_flat = jnp.concatenate([blurred, raw.reshape(plane_count, flat_count)], axis=0)
    both_in = lax.all_to_all(both_flat, "scan", split_axis=1, concat_axis=0, tiled=True)
    both_in = both_in.reshape(lax.axis_size("scan"), 2, plane_count, -1)
    pencil = both_in[:, 0].reshape(offsets.shape[0], -1)
    raw_pencil = both_in[:, 1].reshape(offsets.shape[0], -1)
    predicted_pencil = jnp.dot(sheet_psf, pencil, precision=highest_mode)
    misfit_pencil = predicted_pencil - raw_pencil
    scan_count = lax.axis_size("scan")
    all_planes = offsets.shape[0]
    keep = jnp.eye(all_planes, dtype=jnp.float32).reshape(scan_count, 1, plane_count, all_planes)
    spread = sheet_psf.T.reshape(scan_count, 1, plane_count, all_planes)
    joint = jnp.concatenate([keep, spread], axis=1).reshape(2 * all_planes, all_planes)
    both_pencil = jnp.dot(joint, misfit_pencil, precision=high_mode)
    both_out = lax.all_to_all(both_pencil, "scan", split_axis=0, concat_axis=1, tiled=True)
    misfit = both_out[:plane_count]
    back_volume = both_out[plane_count:].reshape(plane_count, row_count, width_count)
    shrink_level = step_size[0] * threshold[0]

    def shrink(values):
        return jnp.sign(values) * jnp.maximum(jnp.abs(values) - shrink_level, 0.0)

    if lax.axis_size("row") == 2:
        first = lax.axis_index("row") == 0
        edge_start = jnp.where(first, row_count - halo_rows, 0)
        sent = lax.dynamic_slice_in_dim(back_volume, edge_start, halo_rows, axis=1)
        arrived = lax.ppermute(sent, "row", [(0, 1), (1, 0)])
        own = lateral_apply(back_band[:, halo_rows : halo_rows + row_count], back_volume, high_mode)
        stepped = estimate - step_size[0] * own
        finished = shrink(stepped)
        edge = jnp.where(
            first,
            back_band[row_count - halo_rows :, halo_rows + row_count :],
            back_band[:halo_rows, :halo_rows],
        )
        edge_rows = lax.dynamic_slice_in_dim(stepped, edge_start, halo_rows, axis=1)
        edge_rows = edge_rows - step_size[0] * lateral_apply(edge, arrived, high_mode)
        new_estimate = lax.dynamic_update_slice_in_dim(finished, shrink(edge_rows), edge_start, axis=1)
    else:
        gradient = blur_rows(back_band, back_volume, "row", halo_rows, high_mode)
        new_estimate = shrink(estimate - step_size[0] * gradient)
    return (new_estimate, misfit.reshape(plane_count, row_count, width_count))


def solution(mesh):
    placed = (P("scan", "row", None), P("scan", "row", None), P(), P(), P(), P(), P())
    return jax.shard_map(
        body,
        mesh=mesh,
        in_specs=placed,
        out_specs=(P("scan", "row", None), P("scan", "row", None)),
        check_vma=False,
    )
```

```python
import jax
import jax.numpy as jnp
from jax import lax
from jax.sharding import PartitionSpec as P

highest_mode = lax.Precision.HIGHEST
high_mode = lax.Precision.HIGH


def blur_rows(band, cells, axis, width, precision=highest_mode):
    count = lax.axis_size(axis)
    rows = cells.shape[1]
    summed = lateral_apply(band[:, width : width + rows], cells, precision)
    if count == 2:
        first = lax.axis_index(axis) == 0
        sent = lax.dynamic_slice_in_dim(cells, jnp.where(first, rows - width, 0), width, axis=1)
        arrived = lax.ppermute(sent, axis, [(0, 1), (1, 0)])
        edge = jnp.where(first, band[:, width + rows :], band[:, :width])
        return summed + lateral_apply(edge, arrived, precision)
    ends = count - 1
    head = lax.slice_in_dim(cells, 0, width, axis=1)
    tail = lax.slice_in_dim(cells, rows - width, rows, axis=1)
    above = lax.ppermute(tail, axis, [(i, (i + 1) % count) for i in range(ends)])
    below = lax.ppermute(head, axis, [((i + 1) % count, i) for i in range(ends)])
    summed = summed + lateral_apply(band[:, :width], above, precision)
    return summed + lateral_apply(band[:, width + rows :], below, precision)


def band_matrix(kernel_taps, row_count, flip):
    tap_count = kernel_taps.shape[0]
    out_rows = jnp.arange(row_count, dtype=jnp.int32)[:, None]
    in_rows = jnp.arange(row_count + tap_count - 1, dtype=jnp.int32)[None, :]
    lag = in_rows - out_rows
    if flip:
        lag = (tap_count - 1) - lag
    taps = jnp.arange(tap_count, dtype=jnp.int32)
    return jnp.sum(jnp.where(lag[:, :, None] == taps, kernel_taps, 0.0), axis=-1)


def lateral_apply(band, padded, precision=highest_mode):
    return jnp.einsum("rk,pkc->prc", band, padded, precision=precision)


def sheet_matrix(own_offsets, depth_psf, column_count):
    plane_rows = jnp.arange(own_offsets.shape[0], dtype=jnp.int32)[:, None]
    plane_columns = jnp.arange(column_count, dtype=jnp.int32)[None, :]
    lag_planes = plane_columns - plane_rows - own_offsets[:, None]
    depth_count = depth_psf.shape[0]
    inside = (lag_planes >= 0) & (lag_planes < depth_count)
    taps = jnp.arange(depth_count, dtype=jnp.int32)
    picked = jnp.where(lag_planes[:, :, None] == taps, depth_psf, 0.0)
    return jnp.where(inside, jnp.sum(picked, axis=-1), 0.0)


def transpose_apply(sheet_psf, values):
    return lax.dot_general(sheet_psf, values, (((0,), (0,)), ((), ())), precision=highest_mode)


def body(estimate, raw, offsets, depth_psf, lateral_psf, step_size, threshold):
    plane_count, row_count, width_count = estimate.shape
    flat_count = row_count * width_count
    halo_rows = lateral_psf.shape[0] // 2
    sheet_psf = sheet_matrix(offsets, depth_psf, offsets.shape[0])
    blur_band = band_matrix(lateral_psf, row_count, False)
    back_band = band_matrix(lateral_psf, row_count, True)
    blurred = blur_rows(blur_band, estimate, "row", halo_rows).reshape(plane_count, flat_count)
    both_flat = jnp.concatenate([blurred, raw.reshape(plane_count, flat_count)], axis=0)
    both_in = lax.all_to_all(both_flat, "scan", split_axis=1, concat_axis=0, tiled=True)
    both_in = both_in.reshape(lax.axis_size("scan"), 2, plane_count, -1)
    pencil = both_in[:, 0].reshape(offsets.shape[0], -1)
    raw_pencil = both_in[:, 1].reshape(offsets.shape[0], -1)
    predicted_pencil = jnp.dot(sheet_psf, pencil, precision=highest_mode)
    misfit_pencil = predicted_pencil - raw_pencil
    scan_count = lax.axis_size("scan")
    all_planes = offsets.shape[0]
    keep = jnp.eye(all_planes, dtype=jnp.float32).reshape(scan_count, 1, plane_count, all_planes)
    spread = sheet_psf.T.reshape(scan_count, 1, plane_count, all_planes)
    joint = jnp.concatenate([keep, spread], axis=1).reshape(2 * all_planes, all_planes)
    both_pencil = jnp.dot(joint, misfit_pencil, precision=high_mode)
    both_out = lax.all_to_all(both_pencil, "scan", split_axis=0, concat_axis=1, tiled=True)
    misfit = both_out[:plane_count]
    back_volume = both_out[plane_count:].reshape(plane_count, row_count, width_count)
    shrink_level = step_size[0] * threshold[0]

    def shrink(values):
        return jnp.sign(values) * jnp.maximum(jnp.abs(values) - shrink_level, 0.0)

    if lax.axis_size("row") == 2:
        first = lax.axis_index("row") == 0
        edge_start = jnp.where(first, row_count - halo_rows, 0)
        sent = lax.dynamic_slice_in_dim(back_volume, edge_start, halo_rows, axis=1)
        arrived = lax.ppermute(sent, "row", [(0, 1), (1, 0)])
        own = lateral_apply(back_band[:, halo_rows : halo_rows + row_count], back_volume, high_mode)
        stepped = estimate - step_size[0] * own
        finished = shrink(stepped)
        edge = jnp.where(
            first,
            back_band[row_count - halo_rows :, halo_rows + row_count :],
            back_band[:halo_rows, :halo_rows],
        )
        edge_part = lateral_apply(edge, arrived, high_mode)
        edge_full = lax.dynamic_update_slice_in_dim(jnp.zeros_like(stepped), edge_part, edge_start, axis=1)
        row_ids = jnp.arange(row_count, dtype=jnp.int32)[None, :, None]
        at_edge = (row_ids >= edge_start) & (row_ids < edge_start + halo_rows)
        new_estimate = jnp.where(at_edge, shrink(stepped - step_size[0] * edge_full), finished)
    else:
        gradient = blur_rows(back_band, back_volume, "row", halo_rows, high_mode)
        new_estimate = shrink(estimate - step_size[0] * gradient)
    return (new_estimate, misfit.reshape(plane_count, row_count, width_count))


def solution(mesh):
    placed = (P("scan", "row", None), P("scan", "row", None), P(), P(), P(), P(), P())
    return jax.shard_map(
        body,
        mesh=mesh,
        in_specs=placed,
        out_specs=(P("scan", "row", None), P("scan", "row", None)),
        check_vma=False,
    )
```

```python
import jax
import jax.numpy as jnp
from jax import lax
from jax.sharding import PartitionSpec as P

highest_mode = lax.Precision.HIGHEST
high_mode = lax.Precision.HIGH


def blur_rows(band, cells, axis, width, precision=highest_mode):
    count = lax.axis_size(axis)
    rows = cells.shape[1]
    summed = lateral_apply(band[:, width : width + rows], cells, precision)
    if count == 2:
        first = lax.axis_index(axis) == 0
        sent = lax.dynamic_slice_in_dim(cells, jnp.where(first, rows - width, 0), width, axis=1)
        arrived = lax.ppermute(sent, axis, [(0, 1), (1, 0)])
        edge = jnp.where(first, band[:, width + rows :], band[:, :width])
        return summed + lateral_apply(edge, arrived, precision)
    ends = count - 1
    head = lax.slice_in_dim(cells, 0, width, axis=1)
    tail = lax.slice_in_dim(cells, rows - width, rows, axis=1)
    above = lax.ppermute(tail, axis, [(i, (i + 1) % count) for i in range(ends)])
    below = lax.ppermute(head, axis, [((i + 1) % count, i) for i in range(ends)])
    summed = summed + lateral_apply(band[:, :width], above, precision)
    return summed + lateral_apply(band[:, width + rows :], below, precision)


def band_matrix(kernel_taps, row_count, flip):
    tap_count = kernel_taps.shape[0]
    out_rows = jnp.arange(row_count, dtype=jnp.int32)[:, None]
    in_rows = jnp.arange(row_count + tap_count - 1, dtype=jnp.int32)[None, :]
    lag = in_rows - out_rows
    if flip:
        lag = (tap_count - 1) - lag
    taps = jnp.arange(tap_count, dtype=jnp.int32)
    return jnp.sum(jnp.where(lag[:, :, None] == taps, kernel_taps, 0.0), axis=-1)


def lateral_apply(band, padded, precision=highest_mode):
    return jnp.einsum("rk,pkc->prc", band, padded, precision=precision)


def sheet_matrix(own_offsets, depth_psf, column_count):
    plane_rows = jnp.arange(own_offsets.shape[0], dtype=jnp.int32)[:, None]
    plane_columns = jnp.arange(column_count, dtype=jnp.int32)[None, :]
    lag_planes = plane_columns - plane_rows - own_offsets[:, None]
    depth_count = depth_psf.shape[0]
    inside = (lag_planes >= 0) & (lag_planes < depth_count)
    taps = jnp.arange(depth_count, dtype=jnp.int32)
    picked = jnp.where(lag_planes[:, :, None] == taps, depth_psf, 0.0)
    return jnp.where(inside, jnp.sum(picked, axis=-1), 0.0)


def transpose_apply(sheet_psf, values):
    return lax.dot_general(sheet_psf, values, (((0,), (0,)), ((), ())), precision=highest_mode)


def body(estimate, raw, offsets, depth_psf, lateral_psf, step_size, threshold):
    plane_count, row_count, width_count = estimate.shape
    flat_count = row_count * width_count
    halo_rows = lateral_psf.shape[0] // 2
    sheet_psf = sheet_matrix(offsets, depth_psf, offsets.shape[0])
    blur_band = band_matrix(lateral_psf, row_count, False)
    back_band = band_matrix(lateral_psf, row_count, True)
    blurred = blur_rows(blur_band, estimate, "row", halo_rows).reshape(plane_count, flat_count)
    both_flat = jnp.concatenate([blurred, raw.reshape(plane_count, flat_count)], axis=0)
    both_in = lax.all_to_all(both_flat, "scan", split_axis=1, concat_axis=0, tiled=True)
    both_in = both_in.reshape(lax.axis_size("scan"), 2, plane_count, -1)
    pencil = both_in[:, 0].reshape(offsets.shape[0], -1)
    raw_pencil = both_in[:, 1].reshape(offsets.shape[0], -1)
    predicted_pencil = jnp.dot(sheet_psf, pencil, precision=highest_mode)
    misfit_pencil = predicted_pencil - raw_pencil
    scan_count = lax.axis_size("scan")
    all_planes = offsets.shape[0]
    keep = jnp.eye(all_planes, dtype=jnp.float32).reshape(scan_count, 1, plane_count, all_planes)
    spread = sheet_psf.T.reshape(scan_count, 1, plane_count, all_planes)
    joint = jnp.concatenate([keep, spread], axis=1).reshape(2 * all_planes, all_planes)
    both_pencil = jnp.dot(joint, misfit_pencil, precision=high_mode)
    both_out = lax.all_to_all(both_pencil, "scan", split_axis=0, concat_axis=1, tiled=True)
    misfit = both_out[:plane_count]
    back_volume = both_out[plane_count:].reshape(plane_count, row_count, width_count)
    shrink_level = step_size[0] * threshold[0]

    def shrink(values):
        return jnp.sign(values) * jnp.maximum(jnp.abs(values) - shrink_level, 0.0)

    if lax.axis_size("row") == 2:
        first = lax.axis_index("row") == 0
        edge_start = jnp.where(first, row_count - halo_rows, 0)
        sent = lax.dynamic_slice_in_dim(back_volume, edge_start, halo_rows, axis=1)
        arrived = lax.ppermute(sent, "row", [(0, 1), (1, 0)])
        own = lateral_apply(back_band[:, halo_rows : halo_rows + row_count], back_volume, high_mode)
        stepped = estimate - step_size[0] * own
        finished = shrink(stepped)
        finished, stepped = lax.optimization_barrier((finished, stepped))
        edge = jnp.where(
            first,
            back_band[row_count - halo_rows :, halo_rows + row_count :],
            back_band[:halo_rows, :halo_rows],
        )
        edge_part = lateral_apply(edge, arrived, high_mode)
        edge_full = lax.dynamic_update_slice_in_dim(jnp.zeros_like(stepped), edge_part, edge_start, axis=1)
        row_ids = jnp.arange(row_count, dtype=jnp.int32)[None, :, None]
        at_edge = (row_ids >= edge_start) & (row_ids < edge_start + halo_rows)
        new_estimate = jnp.where(at_edge, shrink(stepped - step_size[0] * edge_full), finished)
    else:
        gradient = blur_rows(back_band, back_volume, "row", halo_rows, high_mode)
        new_estimate = shrink(estimate - step_size[0] * gradient)
    return (new_estimate, misfit.reshape(plane_count, row_count, width_count))


def solution(mesh):
    placed = (P("scan", "row", None), P("scan", "row", None), P(), P(), P(), P(), P())
    return jax.shard_map(
        body,
        mesh=mesh,
        in_specs=placed,
        out_specs=(P("scan", "row", None), P("scan", "row", None)),
        check_vma=False,
    )
```

```python
import jax
import jax.numpy as jnp
from jax import lax
from jax.sharding import PartitionSpec as P

highest_mode = lax.Precision.HIGHEST
high_mode = lax.Precision.HIGH


def blur_rows(band, cells, axis, width, precision=highest_mode):
    count = lax.axis_size(axis)
    rows = cells.shape[1]
    summed = lateral_apply(band[:, width : width + rows], cells, precision)
    if count == 2:
        first = lax.axis_index(axis) == 0
        sent = lax.dynamic_slice_in_dim(cells, jnp.where(first, rows - width, 0), width, axis=1)
        arrived = lax.ppermute(sent, axis, [(0, 1), (1, 0)])
        edge = jnp.where(first, band[:, width + rows :], band[:, :width])
        return summed + lateral_apply(edge, arrived, precision)
    ends = count - 1
    head = lax.slice_in_dim(cells, 0, width, axis=1)
    tail = lax.slice_in_dim(cells, rows - width, rows, axis=1)
    above = lax.ppermute(tail, axis, [(i, (i + 1) % count) for i in range(ends)])
    below = lax.ppermute(head, axis, [((i + 1) % count, i) for i in range(ends)])
    summed = summed + lateral_apply(band[:, :width], above, precision)
    return summed + lateral_apply(band[:, width + rows :], below, precision)


def band_matrix(kernel_taps, row_count, flip):
    tap_count = kernel_taps.shape[0]
    out_rows = jnp.arange(row_count, dtype=jnp.int32)[:, None]
    in_rows = jnp.arange(row_count + tap_count - 1, dtype=jnp.int32)[None, :]
    lag = in_rows - out_rows
    if flip:
        lag = (tap_count - 1) - lag
    taps = jnp.arange(tap_count, dtype=jnp.int32)
    return jnp.sum(jnp.where(lag[:, :, None] == taps, kernel_taps, 0.0), axis=-1)


def lateral_apply(band, padded, precision=highest_mode):
    return jnp.einsum("rk,pkc->prc", band, padded, precision=precision)


def sheet_matrix(own_offsets, depth_psf, column_count):
    plane_rows = jnp.arange(own_offsets.shape[0], dtype=jnp.int32)[:, None]
    plane_columns = jnp.arange(column_count, dtype=jnp.int32)[None, :]
    lag_planes = plane_columns - plane_rows - own_offsets[:, None]
    depth_count = depth_psf.shape[0]
    inside = (lag_planes >= 0) & (lag_planes < depth_count)
    taps = jnp.arange(depth_count, dtype=jnp.int32)
    picked = jnp.where(lag_planes[:, :, None] == taps, depth_psf, 0.0)
    return jnp.where(inside, jnp.sum(picked, axis=-1), 0.0)


def transpose_apply(sheet_psf, values):
    return lax.dot_general(sheet_psf, values, (((0,), (0,)), ((), ())), precision=highest_mode)


def body(estimate, raw, offsets, depth_psf, lateral_psf, step_size, threshold):
    plane_count, row_count, width_count = estimate.shape
    flat_count = row_count * width_count
    halo_rows = lateral_psf.shape[0] // 2
    sheet_psf = sheet_matrix(offsets, depth_psf, offsets.shape[0])
    blur_band = band_matrix(lateral_psf, row_count, False)
    back_band = band_matrix(lateral_psf, row_count, True)
    if lax.axis_size("row") == 2:
        first_row = lax.axis_index("row") == 0
        front_start = jnp.where(first_row, row_count - halo_rows, 0)
        front_sent = lax.dynamic_slice_in_dim(estimate, front_start, halo_rows, axis=1)
        front_arrived = lax.ppermute(front_sent, "row", [(0, 1), (1, 0)])
        own_blur = lateral_apply(blur_band[:, halo_rows : halo_rows + row_count], estimate)
        front_edge = jnp.where(
            first_row,
            blur_band[row_count - halo_rows :, halo_rows + row_count :],
            blur_band[:halo_rows, :halo_rows],
        )
        edge_rows = lax.dynamic_slice_in_dim(own_blur, front_start, halo_rows, axis=1)
        edge_rows = edge_rows + lateral_apply(front_edge, front_arrived)
        blurred = lax.dynamic_update_slice_in_dim(own_blur, edge_rows, front_start, axis=1)
        blurred = blurred.reshape(plane_count, flat_count)
    else:
        blurred = blur_rows(blur_band, estimate, "row", halo_rows).reshape(plane_count, flat_count)
    both_flat = jnp.concatenate([blurred, raw.reshape(plane_count, flat_count)], axis=0)
    both_in = lax.all_to_all(both_flat, "scan", split_axis=1, concat_axis=0, tiled=True)
    both_in = both_in.reshape(lax.axis_size("scan"), 2, plane_count, -1)
    pencil = both_in[:, 0].reshape(offsets.shape[0], -1)
    raw_pencil = both_in[:, 1].reshape(offsets.shape[0], -1)
    predicted_pencil = jnp.dot(sheet_psf, pencil, precision=highest_mode)
    misfit_pencil = predicted_pencil - raw_pencil
    scan_count = lax.axis_size("scan")
    all_planes = offsets.shape[0]
    keep = jnp.eye(all_planes, dtype=jnp.float32).reshape(scan_count, 1, plane_count, all_planes)
    spread = sheet_psf.T.reshape(scan_count, 1, plane_count, all_planes)
    joint = jnp.concatenate([keep, spread], axis=1).reshape(2 * all_planes, all_planes)
    both_pencil = jnp.dot(joint, misfit_pencil, precision=high_mode)
    both_out = lax.all_to_all(both_pencil, "scan", split_axis=0, concat_axis=1, tiled=True)
    misfit = both_out[:plane_count]
    back_volume = both_out[plane_count:].reshape(plane_count, row_count, width_count)
    shrink_level = step_size[0] * threshold[0]

    def shrink(values):
        return jnp.sign(values) * jnp.maximum(jnp.abs(values) - shrink_level, 0.0)

    if lax.axis_size("row") == 2:
        first = lax.axis_index("row") == 0
        edge_start = jnp.where(first, row_count - halo_rows, 0)
        sent = lax.dynamic_slice_in_dim(back_volume, edge_start, halo_rows, axis=1)
        arrived = lax.ppermute(sent, "row", [(0, 1), (1, 0)])
        own = lateral_apply(back_band[:, halo_rows : halo_rows + row_count], back_volume, high_mode)
        stepped = estimate - step_size[0] * own
        finished = shrink(stepped)
        edge = jnp.where(
            first,
            back_band[row_count - halo_rows :, halo_rows + row_count :],
            back_band[:halo_rows, :halo_rows],
        )
        edge_rows = lax.dynamic_slice_in_dim(stepped, edge_start, halo_rows, axis=1)
        edge_rows = edge_rows - step_size[0] * lateral_apply(edge, arrived, high_mode)
        new_estimate = lax.dynamic_update_slice_in_dim(finished, shrink(edge_rows), edge_start, axis=1)
    else:
        gradient = blur_rows(back_band, back_volume, "row", halo_rows, high_mode)
        new_estimate = shrink(estimate - step_size[0] * gradient)
    return (new_estimate, misfit.reshape(plane_count, row_count, width_count))


def solution(mesh):
    placed = (P("scan", "row", None), P("scan", "row", None), P(), P(), P(), P(), P())
    return jax.shard_map(
        body,
        mesh=mesh,
        in_specs=placed,
        out_specs=(P("scan", "row", None), P("scan", "row", None)),
        check_vma=False,
    )
```

```python
import jax
import jax.numpy as jnp
from jax import lax
from jax.sharding import PartitionSpec as P

highest_mode = lax.Precision.HIGHEST
high_mode = lax.Precision.HIGH


def blur_rows(band, cells, axis, width, precision=highest_mode):
    count = lax.axis_size(axis)
    rows = cells.shape[1]
    summed = lateral_apply(band[:, width : width + rows], cells, precision)
    if count == 2:
        first = lax.axis_index(axis) == 0
        sent = lax.dynamic_slice_in_dim(cells, jnp.where(first, rows - width, 0), width, axis=1)
        arrived = lax.ppermute(sent, axis, [(0, 1), (1, 0)])
        edge = jnp.where(first, band[:, width + rows :], band[:, :width])
        return summed + lateral_apply(edge, arrived, precision)
    ends = count - 1
    head = lax.slice_in_dim(cells, 0, width, axis=1)
    tail = lax.slice_in_dim(cells, rows - width, rows, axis=1)
    above = lax.ppermute(tail, axis, [(i, (i + 1) % count) for i in range(ends)])
    below = lax.ppermute(head, axis, [((i + 1) % count, i) for i in range(ends)])
    summed = summed + lateral_apply(band[:, :width], above, precision)
    return summed + lateral_apply(band[:, width + rows :], below, precision)


def band_matrix(kernel_taps, row_count, flip):
    tap_count = kernel_taps.shape[0]
    out_rows = jnp.arange(row_count, dtype=jnp.int32)[:, None]
    in_rows = jnp.arange(row_count + tap_count - 1, dtype=jnp.int32)[None, :]
    lag = in_rows - out_rows
    if flip:
        lag = (tap_count - 1) - lag
    taps = jnp.arange(tap_count, dtype=jnp.int32)
    return jnp.sum(jnp.where(lag[:, :, None] == taps, kernel_taps, 0.0), axis=-1)


def lateral_apply(band, padded, precision=highest_mode):
    return jnp.einsum("rk,pkc->prc", band, padded, precision=precision)


def sheet_matrix(own_offsets, depth_psf, column_count):
    plane_rows = jnp.arange(own_offsets.shape[0], dtype=jnp.int32)[:, None]
    plane_columns = jnp.arange(column_count, dtype=jnp.int32)[None, :]
    lag_planes = plane_columns - plane_rows - own_offsets[:, None]
    depth_count = depth_psf.shape[0]
    inside = (lag_planes >= 0) & (lag_planes < depth_count)
    taps = jnp.arange(depth_count, dtype=jnp.int32)
    picked = jnp.where(lag_planes[:, :, None] == taps, depth_psf, 0.0)
    return jnp.where(inside, jnp.sum(picked, axis=-1), 0.0)


def transpose_apply(sheet_psf, values):
    return lax.dot_general(sheet_psf, values, (((0,), (0,)), ((), ())), precision=highest_mode)


def body(estimate, raw, offsets, depth_psf, lateral_psf, step_size, threshold):
    plane_count, row_count, width_count = estimate.shape
    flat_count = row_count * width_count
    halo_rows = lateral_psf.shape[0] // 2
    sheet_psf = sheet_matrix(offsets, depth_psf, offsets.shape[0])
    blur_band = band_matrix(lateral_psf, row_count, False)
    back_band = band_matrix(lateral_psf, row_count, True)
    scan_count = lax.axis_size("scan")
    per_chunk = row_count // scan_count if row_count % scan_count == 0 else 0
    if lax.axis_size("row") == 2 and per_chunk and halo_rows % per_chunk == 0:
        first_row = lax.axis_index("row") == 0
        front_start = jnp.where(first_row, row_count - halo_rows, 0)
        front_sent = lax.dynamic_slice_in_dim(estimate, front_start, halo_rows, axis=1)
        front_arrived = lax.ppermute(front_sent, "row", [(0, 1), (1, 0)])
        own_blur = lateral_apply(blur_band[:, halo_rows : halo_rows + row_count], estimate)
        front_edge = jnp.where(
            first_row,
            blur_band[row_count - halo_rows :, halo_rows + row_count :],
            blur_band[:halo_rows, :halo_rows],
        )
        edge_rows = lax.dynamic_slice_in_dim(own_blur, front_start, halo_rows, axis=1)
        edge_rows = edge_rows + lateral_apply(front_edge, front_arrived)

        def chunked(volume):
            return volume.reshape(plane_count, scan_count, flat_count // scan_count).transpose(1, 0, 2)

        both_chunks = jnp.concatenate([chunked(own_blur), chunked(raw)], axis=1)
        halo_chunks = halo_rows // per_chunk
        edge_chunks = edge_rows.reshape(plane_count, halo_chunks, flat_count // scan_count).transpose(1, 0, 2)
        both_chunks = lax.dynamic_update_slice_in_dim(both_chunks, edge_chunks, front_start // per_chunk, axis=0)
        both_in = lax.all_to_all(both_chunks, "scan", split_axis=0, concat_axis=0, tiled=True)
        both_in = both_in.reshape(scan_count, 2, plane_count, -1)
    else:
        blurred = blur_rows(blur_band, estimate, "row", halo_rows).reshape(plane_count, flat_count)
        both_flat = jnp.concatenate([blurred, raw.reshape(plane_count, flat_count)], axis=0)
        both_in = lax.all_to_all(both_flat, "scan", split_axis=1, concat_axis=0, tiled=True)
        both_in = both_in.reshape(scan_count, 2, plane_count, -1)
    pencil = both_in[:, 0].reshape(offsets.shape[0], -1)
    raw_pencil = both_in[:, 1].reshape(offsets.shape[0], -1)
    predicted_pencil = jnp.dot(sheet_psf, pencil, precision=highest_mode)
    misfit_pencil = predicted_pencil - raw_pencil
    scan_count = lax.axis_size("scan")
    all_planes = offsets.shape[0]
    keep = jnp.eye(all_planes, dtype=jnp.float32).reshape(scan_count, 1, plane_count, all_planes)
    spread = sheet_psf.T.reshape(scan_count, 1, plane_count, all_planes)
    joint = jnp.concatenate([keep, spread], axis=1).reshape(2 * all_planes, all_planes)
    both_pencil = jnp.dot(joint, misfit_pencil, precision=high_mode)
    both_out = lax.all_to_all(both_pencil, "scan", split_axis=0, concat_axis=1, tiled=True)
    misfit = both_out[:plane_count]
    back_volume = both_out[plane_count:].reshape(plane_count, row_count, width_count)
    shrink_level = step_size[0] * threshold[0]

    def shrink(values):
        return jnp.sign(values) * jnp.maximum(jnp.abs(values) - shrink_level, 0.0)

    if lax.axis_size("row") == 2:
        first = lax.axis_index("row") == 0
        edge_start = jnp.where(first, row_count - halo_rows, 0)
        sent = lax.dynamic_slice_in_dim(back_volume, edge_start, halo_rows, axis=1)
        arrived = lax.ppermute(sent, "row", [(0, 1), (1, 0)])
        own = lateral_apply(back_band[:, halo_rows : halo_rows + row_count], back_volume, high_mode)
        stepped = estimate - step_size[0] * own
        finished = shrink(stepped)
        edge = jnp.where(
            first,
            back_band[row_count - halo_rows :, halo_rows + row_count :],
            back_band[:halo_rows, :halo_rows],
        )
        edge_rows = lax.dynamic_slice_in_dim(stepped, edge_start, halo_rows, axis=1)
        edge_rows = edge_rows - step_size[0] * lateral_apply(edge, arrived, high_mode)
        new_estimate = lax.dynamic_update_slice_in_dim(finished, shrink(edge_rows), edge_start, axis=1)
    else:
        gradient = blur_rows(back_band, back_volume, "row", halo_rows, high_mode)
        new_estimate = shrink(estimate - step_size[0] * gradient)
    return (new_estimate, misfit.reshape(plane_count, row_count, width_count))


def solution(mesh):
    placed = (P("scan", "row", None), P("scan", "row", None), P(), P(), P(), P(), P())
    return jax.shard_map(
        body,
        mesh=mesh,
        in_specs=placed,
        out_specs=(P("scan", "row", None), P("scan", "row", None)),
        check_vma=False,
    )
```

```python
import jax
import jax.numpy as jnp
from jax import lax
from jax.sharding import PartitionSpec as P

highest_mode = lax.Precision.HIGHEST
high_mode = lax.Precision.HIGH


def blur_rows(band, cells, axis, width, precision=highest_mode):
    count = lax.axis_size(axis)
    rows = cells.shape[1]
    summed = lateral_apply(band[:, width : width + rows], cells, precision)
    if count == 2:
        first = lax.axis_index(axis) == 0
        sent = lax.dynamic_slice_in_dim(cells, jnp.where(first, rows - width, 0), width, axis=1)
        arrived = lax.ppermute(sent, axis, [(0, 1), (1, 0)])
        edge = jnp.where(first, band[:, width + rows :], band[:, :width])
        return summed + lateral_apply(edge, arrived, precision)
    ends = count - 1
    head = lax.slice_in_dim(cells, 0, width, axis=1)
    tail = lax.slice_in_dim(cells, rows - width, rows, axis=1)
    above = lax.ppermute(tail, axis, [(i, (i + 1) % count) for i in range(ends)])
    below = lax.ppermute(head, axis, [((i + 1) % count, i) for i in range(ends)])
    summed = summed + lateral_apply(band[:, :width], above, precision)
    return summed + lateral_apply(band[:, width + rows :], below, precision)


def band_matrix(kernel_taps, row_count, flip):
    tap_count = kernel_taps.shape[0]
    out_rows = jnp.arange(row_count, dtype=jnp.int32)[:, None]
    in_rows = jnp.arange(row_count + tap_count - 1, dtype=jnp.int32)[None, :]
    lag = in_rows - out_rows
    if flip:
        lag = (tap_count - 1) - lag
    taps = jnp.arange(tap_count, dtype=jnp.int32)
    return jnp.sum(jnp.where(lag[:, :, None] == taps, kernel_taps, 0.0), axis=-1)


def lateral_apply(band, padded, precision=highest_mode):
    return jnp.einsum("rk,pkc->prc", band, padded, precision=precision)


def sheet_matrix(own_offsets, depth_psf, column_count):
    plane_rows = jnp.arange(own_offsets.shape[0], dtype=jnp.int32)[:, None]
    plane_columns = jnp.arange(column_count, dtype=jnp.int32)[None, :]
    lag_planes = plane_columns - plane_rows - own_offsets[:, None]
    depth_count = depth_psf.shape[0]
    inside = (lag_planes >= 0) & (lag_planes < depth_count)
    taps = jnp.arange(depth_count, dtype=jnp.int32)
    picked = jnp.where(lag_planes[:, :, None] == taps, depth_psf, 0.0)
    return jnp.where(inside, jnp.sum(picked, axis=-1), 0.0)


def transpose_apply(sheet_psf, values):
    return lax.dot_general(sheet_psf, values, (((0,), (0,)), ((), ())), precision=highest_mode)


def body(estimate, raw, offsets, depth_psf, lateral_psf, step_size, threshold):
    plane_count, row_count, width_count = estimate.shape
    flat_count = row_count * width_count
    halo_rows = lateral_psf.shape[0] // 2
    sheet_psf = sheet_matrix(offsets, depth_psf, offsets.shape[0])
    blur_band = band_matrix(lateral_psf, row_count, False)
    back_band = band_matrix(lateral_psf, row_count, True)
    if lax.axis_size("row") == 2:
        first_row = lax.axis_index("row") == 0
        front_start = jnp.where(first_row, row_count - halo_rows, 0)
        front_sent = lax.dynamic_slice_in_dim(estimate, front_start, halo_rows, axis=1)
        front_arrived = lax.ppermute(front_sent, "row", [(0, 1), (1, 0)])
        own_blur = lateral_apply(blur_band[:, halo_rows : halo_rows + row_count], estimate)
        front_edge = jnp.where(
            first_row,
            blur_band[row_count - halo_rows :, halo_rows + row_count :],
            blur_band[:halo_rows, :halo_rows],
        )
        edge_rows = lax.dynamic_slice_in_dim(own_blur, front_start, halo_rows, axis=1)
        edge_rows = edge_rows + lateral_apply(front_edge, front_arrived)
        blurred = lax.dynamic_update_slice_in_dim(own_blur, edge_rows, front_start, axis=1)
        blurred = blurred.reshape(plane_count, flat_count)
    else:
        blurred = blur_rows(blur_band, estimate, "row", halo_rows).reshape(plane_count, flat_count)
    if row_count % lax.axis_size("scan") == 0:
        both_rows = jnp.concatenate([blurred.reshape(plane_count, row_count, width_count), raw], axis=0)
        both_in = lax.all_to_all(both_rows, "scan", split_axis=1, concat_axis=0, tiled=True)
    else:
        both_flat = jnp.concatenate([blurred, raw.reshape(plane_count, flat_count)], axis=0)
        both_in = lax.all_to_all(both_flat, "scan", split_axis=1, concat_axis=0, tiled=True)
    both_in = both_in.reshape(lax.axis_size("scan"), 2, plane_count, -1)
    pencil = both_in[:, 0].reshape(offsets.shape[0], -1)
    raw_pencil = both_in[:, 1].reshape(offsets.shape[0], -1)
    predicted_pencil = jnp.dot(sheet_psf, pencil, precision=highest_mode)
    misfit_pencil = predicted_pencil - raw_pencil
    scan_count = lax.axis_size("scan")
    all_planes = offsets.shape[0]
    keep = jnp.eye(all_planes, dtype=jnp.float32).reshape(scan_count, 1, plane_count, all_planes)
    spread = sheet_psf.T.reshape(scan_count, 1, plane_count, all_planes)
    joint = jnp.concatenate([keep, spread], axis=1).reshape(2 * all_planes, all_planes)
    both_pencil = jnp.dot(joint, misfit_pencil, precision=high_mode)
    both_out = lax.all_to_all(both_pencil, "scan", split_axis=0, concat_axis=1, tiled=True)
    misfit = both_out[:plane_count]
    back_volume = both_out[plane_count:].reshape(plane_count, row_count, width_count)
    shrink_level = step_size[0] * threshold[0]

    def shrink(values):
        return jnp.sign(values) * jnp.maximum(jnp.abs(values) - shrink_level, 0.0)

    if lax.axis_size("row") == 2:
        first = lax.axis_index("row") == 0
        edge_start = jnp.where(first, row_count - halo_rows, 0)
        sent = lax.dynamic_slice_in_dim(back_volume, edge_start, halo_rows, axis=1)
        arrived = lax.ppermute(sent, "row", [(0, 1), (1, 0)])
        own = lateral_apply(back_band[:, halo_rows : halo_rows + row_count], back_volume, high_mode)
        stepped = estimate - step_size[0] * own
        finished = shrink(stepped)
        edge = jnp.where(
            first,
            back_band[row_count - halo_rows :, halo_rows + row_count :],
            back_band[:halo_rows, :halo_rows],
        )
        edge_rows = lax.dynamic_slice_in_dim(stepped, edge_start, halo_rows, axis=1)
        edge_rows = edge_rows - step_size[0] * lateral_apply(edge, arrived, high_mode)
        new_estimate = lax.dynamic_update_slice_in_dim(finished, shrink(edge_rows), edge_start, axis=1)
    else:
        gradient = blur_rows(back_band, back_volume, "row", halo_rows, high_mode)
        new_estimate = shrink(estimate - step_size[0] * gradient)
    return (new_estimate, misfit.reshape(plane_count, row_count, width_count))


def solution(mesh):
    placed = (P("scan", "row", None), P("scan", "row", None), P(), P(), P(), P(), P())
    return jax.shard_map(
        body,
        mesh=mesh,
        in_specs=placed,
        out_specs=(P("scan", "row", None), P("scan", "row", None)),
        check_vma=False,
    )
```

```python
import jax
import jax.numpy as jnp
from jax import lax
from jax.sharding import PartitionSpec as P

highest_mode = lax.Precision.HIGHEST
high_mode = lax.Precision.HIGH


def blur_rows(band, cells, axis, width, precision=highest_mode):
    count = lax.axis_size(axis)
    rows = cells.shape[1]
    summed = lateral_apply(band[:, width : width + rows], cells, precision)
    if count == 2:
        first = lax.axis_index(axis) == 0
        sent = lax.dynamic_slice_in_dim(cells, jnp.where(first, rows - width, 0), width, axis=1)
        arrived = lax.ppermute(sent, axis, [(0, 1), (1, 0)])
        edge = jnp.where(first, band[:, width + rows :], band[:, :width])
        return summed + lateral_apply(edge, arrived, precision)
    ends = count - 1
    head = lax.slice_in_dim(cells, 0, width, axis=1)
    tail = lax.slice_in_dim(cells, rows - width, rows, axis=1)
    above = lax.ppermute(tail, axis, [(i, (i + 1) % count) for i in range(ends)])
    below = lax.ppermute(head, axis, [((i + 1) % count, i) for i in range(ends)])
    summed = summed + lateral_apply(band[:, :width], above, precision)
    return summed + lateral_apply(band[:, width + rows :], below, precision)


def band_matrix(kernel_taps, row_count, flip):
    tap_count = kernel_taps.shape[0]
    out_rows = jnp.arange(row_count, dtype=jnp.int32)[:, None]
    in_rows = jnp.arange(row_count + tap_count - 1, dtype=jnp.int32)[None, :]
    lag = in_rows - out_rows
    if flip:
        lag = (tap_count - 1) - lag
    band = jnp.zeros(lag.shape, kernel_taps.dtype)
    for tap in range(tap_count):
        band = band + jnp.where(lag == tap, kernel_taps[tap], 0.0)
    return band


def lateral_apply(band, padded, precision=highest_mode):
    return jnp.einsum("rk,pkc->prc", band, padded, precision=precision)


def sheet_matrix(own_offsets, depth_psf, column_count):
    plane_rows = jnp.arange(own_offsets.shape[0], dtype=jnp.int32)[:, None]
    plane_columns = jnp.arange(column_count, dtype=jnp.int32)[None, :]
    lag_planes = plane_columns - plane_rows - own_offsets[:, None]
    depth_count = depth_psf.shape[0]
    inside = (lag_planes >= 0) & (lag_planes < depth_count)
    taps = jnp.arange(depth_count, dtype=jnp.int32)
    picked = jnp.where(lag_planes[:, :, None] == taps, depth_psf, 0.0)
    return jnp.where(inside, jnp.sum(picked, axis=-1), 0.0)


def transpose_apply(sheet_psf, values):
    return lax.dot_general(sheet_psf, values, (((0,), (0,)), ((), ())), precision=highest_mode)


def body(estimate, raw, offsets, depth_psf, lateral_psf, step_size, threshold):
    plane_count, row_count, width_count = estimate.shape
    flat_count = row_count * width_count
    halo_rows = lateral_psf.shape[0] // 2
    sheet_psf = sheet_matrix(offsets, depth_psf, offsets.shape[0])
    blur_band = band_matrix(lateral_psf, row_count, False)
    back_band = band_matrix(lateral_psf, row_count, True)
    if lax.axis_size("row") == 2:
        first_row = lax.axis_index("row") == 0
        front_start = jnp.where(first_row, row_count - halo_rows, 0)
        front_sent = lax.dynamic_slice_in_dim(estimate, front_start, halo_rows, axis=1)
        front_arrived = lax.ppermute(front_sent, "row", [(0, 1), (1, 0)])
        own_blur = lateral_apply(blur_band[:, halo_rows : halo_rows + row_count], estimate)
        front_edge = jnp.where(
            first_row,
            blur_band[row_count - halo_rows :, halo_rows + row_count :],
            blur_band[:halo_rows, :halo_rows],
        )
        edge_rows = lax.dynamic_slice_in_dim(own_blur, front_start, halo_rows, axis=1)
        edge_rows = edge_rows + lateral_apply(front_edge, front_arrived)
        blurred = lax.dynamic_update_slice_in_dim(own_blur, edge_rows, front_start, axis=1)
        blurred = blurred.reshape(plane_count, flat_count)
    else:
        blurred = blur_rows(blur_band, estimate, "row", halo_rows).reshape(plane_count, flat_count)
    both_flat = jnp.concatenate([blurred, raw.reshape(plane_count, flat_count)], axis=0)
    both_in = lax.all_to_all(both_flat, "scan", split_axis=1, concat_axis=0, tiled=True)
    both_in = both_in.reshape(lax.axis_size("scan"), 2, plane_count, -1)
    pencil = both_in[:, 0].reshape(offsets.shape[0], -1)
    raw_pencil = both_in[:, 1].reshape(offsets.shape[0], -1)
    predicted_pencil = jnp.dot(sheet_psf, pencil, precision=highest_mode)
    misfit_pencil = predicted_pencil - raw_pencil
    scan_count = lax.axis_size("scan")
    all_planes = offsets.shape[0]
    keep = jnp.eye(all_planes, dtype=jnp.float32).reshape(scan_count, 1, plane_count, all_planes)
    spread = sheet_psf.T.reshape(scan_count, 1, plane_count, all_planes)
    joint = jnp.concatenate([keep, spread], axis=1).reshape(2 * all_planes, all_planes)
    both_pencil = jnp.dot(joint, misfit_pencil, precision=high_mode)
    both_out = lax.all_to_all(both_pencil, "scan", split_axis=0, concat_axis=1, tiled=True)
    misfit = both_out[:plane_count]
    back_volume = both_out[plane_count:].reshape(plane_count, row_count, width_count)
    shrink_level = step_size[0] * threshold[0]

    def shrink(values):
        return jnp.sign(values) * jnp.maximum(jnp.abs(values) - shrink_level, 0.0)

    if lax.axis_size("row") == 2:
        first = lax.axis_index("row") == 0
        edge_start = jnp.where(first, row_count - halo_rows, 0)
        sent = lax.dynamic_slice_in_dim(back_volume, edge_start, halo_rows, axis=1)
        arrived = lax.ppermute(sent, "row", [(0, 1), (1, 0)])
        own = lateral_apply(back_band[:, halo_rows : halo_rows + row_count], back_volume, high_mode)
        stepped = estimate - step_size[0] * own
        finished = shrink(stepped)
        edge = jnp.where(
            first,
            back_band[row_count - halo_rows :, halo_rows + row_count :],
            back_band[:halo_rows, :halo_rows],
        )
        edge_rows = lax.dynamic_slice_in_dim(stepped, edge_start, halo_rows, axis=1)
        edge_rows = edge_rows - step_size[0] * lateral_apply(edge, arrived, high_mode)
        new_estimate = lax.dynamic_update_slice_in_dim(finished, shrink(edge_rows), edge_start, axis=1)
    else:
        gradient = blur_rows(back_band, back_volume, "row", halo_rows, high_mode)
        new_estimate = shrink(estimate - step_size[0] * gradient)
    return (new_estimate, misfit.reshape(plane_count, row_count, width_count))


def solution(mesh):
    placed = (P("scan", "row", None), P("scan", "row", None), P(), P(), P(), P(), P())
    return jax.shard_map(
        body,
        mesh=mesh,
        in_specs=placed,
        out_specs=(P("scan", "row", None), P("scan", "row", None)),
        check_vma=False,
    )
```

```python
import jax
import jax.numpy as jnp
from jax import lax
from jax.sharding import PartitionSpec as P

highest_mode = lax.Precision.HIGHEST
high_mode = lax.Precision.HIGH


def blur_rows(band, cells, axis, width, precision=highest_mode):
    count = lax.axis_size(axis)
    rows = cells.shape[1]
    summed = lateral_apply(band[:, width : width + rows], cells, precision)
    if count == 2:
        first = lax.axis_index(axis) == 0
        sent = lax.dynamic_slice_in_dim(cells, jnp.where(first, rows - width, 0), width, axis=1)
        arrived = lax.ppermute(sent, axis, [(0, 1), (1, 0)])
        edge = jnp.where(first, band[:, width + rows :], band[:, :width])
        return summed + lateral_apply(edge, arrived, precision)
    ends = count - 1
    head = lax.slice_in_dim(cells, 0, width, axis=1)
    tail = lax.slice_in_dim(cells, rows - width, rows, axis=1)
    above = lax.ppermute(tail, axis, [(i, (i + 1) % count) for i in range(ends)])
    below = lax.ppermute(head, axis, [((i + 1) % count, i) for i in range(ends)])
    summed = summed + lateral_apply(band[:, :width], above, precision)
    return summed + lateral_apply(band[:, width + rows :], below, precision)


def band_matrix(kernel_taps, row_count, flip):
    tap_count = kernel_taps.shape[0]
    out_rows = jnp.arange(row_count, dtype=jnp.int32)[:, None]
    in_rows = jnp.arange(row_count + tap_count - 1, dtype=jnp.int32)[None, :]
    lag = in_rows - out_rows
    if flip:
        lag = (tap_count - 1) - lag
    taps = jnp.arange(tap_count, dtype=jnp.int32)
    return jnp.sum(jnp.where(lag[:, :, None] == taps, kernel_taps, 0.0), axis=-1)


def lateral_apply(band, padded, precision=highest_mode):
    return jnp.einsum("rk,pkc->prc", band, padded, precision=precision)


def sheet_matrix(own_offsets, depth_psf, column_count):
    plane_rows = jnp.arange(own_offsets.shape[0], dtype=jnp.int32)[:, None]
    plane_columns = jnp.arange(column_count, dtype=jnp.int32)[None, :]
    lag_planes = plane_columns - plane_rows - own_offsets[:, None]
    depth_count = depth_psf.shape[0]
    inside = (lag_planes >= 0) & (lag_planes < depth_count)
    taps = jnp.arange(depth_count, dtype=jnp.int32)
    picked = jnp.where(lag_planes[:, :, None] == taps, depth_psf, 0.0)
    return jnp.where(inside, jnp.sum(picked, axis=-1), 0.0)


def transpose_apply(sheet_psf, values):
    return lax.dot_general(sheet_psf, values, (((0,), (0,)), ((), ())), precision=highest_mode)


def body(estimate, raw, offsets, depth_psf, lateral_psf, step_size, threshold):
    plane_count, row_count, width_count = estimate.shape
    flat_count = row_count * width_count
    halo_rows = lateral_psf.shape[0] // 2
    sheet_psf = sheet_matrix(offsets, depth_psf, offsets.shape[0])
    late_taps, sheet_psf = lax.optimization_barrier((lateral_psf, sheet_psf))
    back_band = band_matrix(late_taps, row_count, True)
    blur_band = band_matrix(lateral_psf, row_count, False)
    if lax.axis_size("row") == 2:
        first_row = lax.axis_index("row") == 0
        front_start = jnp.where(first_row, row_count - halo_rows, 0)
        front_sent = lax.dynamic_slice_in_dim(estimate, front_start, halo_rows, axis=1)
        front_arrived = lax.ppermute(front_sent, "row", [(0, 1), (1, 0)])
        own_blur = lateral_apply(blur_band[:, halo_rows : halo_rows + row_count], estimate)
        front_edge = jnp.where(
            first_row,
            blur_band[row_count - halo_rows :, halo_rows + row_count :],
            blur_band[:halo_rows, :halo_rows],
        )
        edge_rows = lax.dynamic_slice_in_dim(own_blur, front_start, halo_rows, axis=1)
        edge_rows = edge_rows + lateral_apply(front_edge, front_arrived)
        blurred = lax.dynamic_update_slice_in_dim(own_blur, edge_rows, front_start, axis=1)
        blurred = blurred.reshape(plane_count, flat_count)
    else:
        blurred = blur_rows(blur_band, estimate, "row", halo_rows).reshape(plane_count, flat_count)
    both_flat = jnp.concatenate([blurred, raw.reshape(plane_count, flat_count)], axis=0)
    both_in = lax.all_to_all(both_flat, "scan", split_axis=1, concat_axis=0, tiled=True)
    both_in = both_in.reshape(lax.axis_size("scan"), 2, plane_count, -1)
    pencil = both_in[:, 0].reshape(offsets.shape[0], -1)
    raw_pencil = both_in[:, 1].reshape(offsets.shape[0], -1)
    predicted_pencil = jnp.dot(sheet_psf, pencil, precision=highest_mode)
    misfit_pencil = predicted_pencil - raw_pencil
    scan_count = lax.axis_size("scan")
    all_planes = offsets.shape[0]
    keep = jnp.eye(all_planes, dtype=jnp.float32).reshape(scan_count, 1, plane_count, all_planes)
    spread = sheet_psf.T.reshape(scan_count, 1, plane_count, all_planes)
    joint = jnp.concatenate([keep, spread], axis=1).reshape(2 * all_planes, all_planes)
    both_pencil = jnp.dot(joint, misfit_pencil, precision=high_mode)
    both_out = lax.all_to_all(both_pencil, "scan", split_axis=0, concat_axis=1, tiled=True)
    misfit = both_out[:plane_count]
    back_volume = both_out[plane_count:].reshape(plane_count, row_count, width_count)
    shrink_level = step_size[0] * threshold[0]

    def shrink(values):
        return jnp.sign(values) * jnp.maximum(jnp.abs(values) - shrink_level, 0.0)

    if lax.axis_size("row") == 2:
        first = lax.axis_index("row") == 0
        edge_start = jnp.where(first, row_count - halo_rows, 0)
        sent = lax.dynamic_slice_in_dim(back_volume, edge_start, halo_rows, axis=1)
        arrived = lax.ppermute(sent, "row", [(0, 1), (1, 0)])
        own = lateral_apply(back_band[:, halo_rows : halo_rows + row_count], back_volume, high_mode)
        stepped = estimate - step_size[0] * own
        finished = shrink(stepped)
        edge = jnp.where(
            first,
            back_band[row_count - halo_rows :, halo_rows + row_count :],
            back_band[:halo_rows, :halo_rows],
        )
        edge_rows = lax.dynamic_slice_in_dim(stepped, edge_start, halo_rows, axis=1)
        edge_rows = edge_rows - step_size[0] * lateral_apply(edge, arrived, high_mode)
        new_estimate = lax.dynamic_update_slice_in_dim(finished, shrink(edge_rows), edge_start, axis=1)
    else:
        gradient = blur_rows(back_band, back_volume, "row", halo_rows, high_mode)
        new_estimate = shrink(estimate - step_size[0] * gradient)
    return (new_estimate, misfit.reshape(plane_count, row_count, width_count))


def solution(mesh):
    placed = (P("scan", "row", None), P("scan", "row", None), P(), P(), P(), P(), P())
    return jax.shard_map(
        body,
        mesh=mesh,
        in_specs=placed,
        out_specs=(P("scan", "row", None), P("scan", "row", None)),
        check_vma=False,
    )
```
